512 devices in a mesh: take: 4 (over y), outer: 16 (over z), inner: 8 (over x, core).
Axes of the slice: x: 4, y: 4, z: 16, core: 2. Of those that a mesh axis runs over, the one named last changes fastest.
Arguments:
- frames: bfloat16 [16, 65536, 256], P('take', ('outer', 'inner')), may hold values from -6 to 6
- conv_weight: bfloat16 [3, 3, 256, 256], replicated, may hold values from -0.21875 to 0.21875
- conv_bias: float32 [3, 256], replicated, may hold values from -1 to 1
- dilations: int32 [3], replicated, may hold values from 1 to 64, as said below
- head_weight: bfloat16 [256, 128], replicated, may hold values from -0.375 to 0.375
- present: int32 [16, 65536], P('take', ('outer', 'inner')), may hold values 0 or 1
- frame_keep: float32 [16, 65536], P('take', ('outer', 'inner')), may hold values from 0.5 to 1
- channel_params: float32 [3, 64], replicated, may hold values from 0 to 2
- head_cotangent: bfloat16 [16, 65536, 128], P('take', ('outer', 'inner')), may hold values from -6 to 6
Outputs:
- filtered_mean: float32 [16, 64, 65536], P('take', None, ('outer', 'inner'))
- head_grad: float32 [256, 128], replicated
The draws below stay inside these ranges and needn't reach their ends.
Inputs may be any that keep to these rules, and one draw needn't show every extreme that they name: `dilations`: every dilation is 1 to 64; some layer has exactly 64 and another exactly 1.
All inputs are finite; a program needn't handle non-finite values. No bound on the sum of `present` on one device may be relied on, other than what follows from the above.
Results may differ from the reference program's by a relative error of at most 0.0048.
Values may be sent and summed in bfloat16 or wider, within the bound.
No kernel may reach another device: no remote copies, remote signals or barrier semaphores. Data moves between devices by JAX's collectives and lax.ppermute only.
A program may use at most 64 MiB of HBM per device.

```python
import jax
import jax.numpy as jnp
from jax import lax

WIDTH = 256
STATE = 64
LAYERS = 3
DMAX = 64
FR_DEV = 512
TAKES = 16
TOTAL = 65536


def draw_frames(key, part):
    shape = (TAKES, TOTAL, WIDTH)
    values = jax.random.truncated_normal(jax.random.fold_in(key, 1), -6.0, 6.0, shape, jnp.float32)
    return values.astype(jnp.bfloat16)


def draw_dilations(key, part):
    values = jax.random.randint(key, (LAYERS,), 1, DMAX + 1)
    order = jax.random.permutation(jax.random.fold_in(key, 1), LAYERS)
    values = values.at[order[0]].set(DMAX)
    values = values.at[order[1]].set(1)
    return values.astype(jnp.int32)


def draw_frame_keep(key, part):
    chance = jax.random.uniform(jax.random.fold_in(key, 1), (TAKES, TOTAL), jnp.float32)
    level = jax.random.uniform(jax.random.fold_in(key, 2), (TAKES, TOTAL), jnp.float32, 0.5, 0.8)
    return jnp.where(chance < 4.0 / TOTAL, level, 1.0).astype(jnp.float32)


def draw_channel_params(key, part):
    pick = jax.random.uniform(jax.random.fold_in(key, 1), (STATE,), jnp.float32)
    fast_share = 0.4
    drift_share = 0.3
    fast = pick < fast_share
    drift = (pick >= fast_share) & (pick < fast_share + drift_share)
    unit = jax.random.uniform(jax.random.fold_in(key, 2), (3, STATE), jnp.float32)
    low_rate = 0.0012
    high_rate = 1.0 / 30.0
    fast_rate = jnp.exp(jnp.log(low_rate) + unit[0] * jnp.log(high_rate / low_rate))
    slow_rate = jnp.exp(jnp.log(0.05 / TOTAL) + unit[0] * jnp.log(4.0))
    fast_noise = fast_rate * fast_rate * (0.3 + 0.7 * unit[1])
    drift_noise = (0.5 + 1.5 * unit[1]) * 2.0 / (float(TOTAL) * float(FR_DEV))
    long_noise = (0.5 + 1.5 * unit[1]) / float(TOTAL) / float(TOTAL)
    scale = 0.5 + 1.5 * unit[2]
    rate = jnp.where(fast, fast_rate, slow_rate)
    noise = jnp.where(fast, fast_noise, jnp.where(drift, drift_noise, long_noise))
    return jnp.stack([rate, noise, scale]).astype(jnp.float32)


def set_ends(entries, key, low, largest):
    longest = entries.shape.index(max(entries.shape))
    spots = []
    for shift in (0, 1):
        where = [jax.random.randint(jax.random.fold_in(key, axis), (), 0, length) for axis, length in enumerate(entries.shape)]
        where[longest] = (where[longest] + shift) % entries.shape[longest]
        spots.append(tuple(where))
    return entries.at[spots[0]].set(low).at[spots[1]].set(largest)


def block_scale(rng, dims, pieces, low, top_value):
    def one(dim, parts):
        heights = jax.random.uniform(jax.random.fold_in(jax.random.fold_in(rng, 6), dim), (parts,), jnp.float32, low / len(pieces), top_value / len(pieces))
        return jnp.repeat(jnp.exp(heights), dims[dim] // parts).reshape((-1,) + (1,) * (len(dims) - dim - 1))

    level = one(*pieces[0])
    for cut in pieces[1:]:
        level = level * one(*cut)
    return level


def normal_values(own_key, extent, spread, limit, cuts=(), kind=jnp.bfloat16):
    values = jax.random.normal(own_key, extent, jnp.float32) * spread
    if len(cuts) > 0:
        values = block_scale(own_key, extent, cuts, -0.22, 0.18) * values
    return jnp.clip(values, min=-limit, max=limit).astype(kind)


def setup_inputs(seed: int = 0) -> dict:
    key_of = jax.random.split(jax.random.key(seed), 10)
    frames = draw_frames(jax.random.fold_in(key_of[9], 71), 0)
    conv_weight = normal_values(key_of[1], (LAYERS, 3, WIDTH, WIDTH), (3 * WIDTH) ** -0.5, 0.21875)
    conv_bias = jnp.clip(jax.random.uniform(key_of[2], (LAYERS, WIDTH), jnp.float32, -1.0, 1.0), -1.0, 1.0)
    dilations = draw_dilations(jax.random.fold_in(key_of[9], 71), 0)
    head_weight = normal_values(key_of[4], (WIDTH, 2 * STATE), WIDTH ** -0.5, 0.375)
    present = set_ends((jax.random.randint(key_of[5], (TAKES, TOTAL), 0, 4) < 3).astype(jnp.int32), jax.random.fold_in(key_of[5], 1), 0, 1)
    frame_keep = draw_frame_keep(jax.random.fold_in(key_of[9], 71), 0)
    channel_params = draw_channel_params(jax.random.fold_in(key_of[9], 71), 0)
    head_cotangent = normal_values(key_of[8], (TAKES, TOTAL, 2 * STATE), 1.0, 6.0, ((0, 4), (1, 128)))
    return dict(frames=frames, conv_weight=conv_weight, conv_bias=conv_bias, dilations=dilations, head_weight=head_weight, present=present, frame_keep=frame_keep, channel_params=channel_params, head_cotangent=head_cotangent)


def combine(early, late):
    a_one, b_one, c_one, e_one, j_one = early
    a_two, b_two, c_two, e_two, j_two = late
    denom = 1.0 + c_one * j_two
    new_a = a_two * a_one / denom
    new_b = a_two * (b_one + c_one * e_two) / denom + b_two
    new_c = a_two * a_two * c_one / denom + c_two
    new_e = a_one * (e_two - j_two * b_one) / denom + e_one
    new_j = a_one * a_one * j_two / denom + j_one
    return (new_a, new_b, new_c, new_e, new_j)


def doubling_prefix(elems, axis):
    length = elems[0].shape[axis]
    result = elems
    offset = 1
    while offset < length:
        moved = []
        for index, item in enumerate(result):
            fill_value = 1.0 if index == 0 else 0.0
            pad_shape = list(item.shape)
            pad_shape[axis] = offset
            fill = jnp.full(pad_shape, fill_value, item.dtype)
            kept = lax.slice_in_dim(item, 0, length - offset, axis=axis)
            moved.append(jnp.concatenate([fill, kept], axis=axis))
        result = combine(tuple(moved), result)
        offset = offset * 2
    return result


def elements(obs, logp, params, present, keep, first):
    rate = params[0][:, None]
    noise = params[1][:, None]
    scale = params[2][:, None]
    trans = jnp.exp(-rate) * keep
    prec = present * scale * jax.nn.softplus(logp)
    denom = 1.0 + noise * prec
    zeros = jnp.zeros_like(obs)
    elem_a = jnp.where(first, zeros, trans / denom)
    elem_b = jnp.where(first, prec * obs / (1.0 + prec), noise * prec * obs / denom)
    elem_c = jnp.where(first, 1.0 / (1.0 + prec), noise / denom)
    elem_e = jnp.where(first, zeros, trans * prec * obs / denom)
    elem_j = jnp.where(first, zeros, trans * trans * prec / denom)
    return (elem_a, elem_b, elem_c, elem_e, elem_j)


def one_take(frames, present, keep, cotangent, conv_weight, conv_bias, dilations, head_weight, params):
    hidden = frames
    length = frames.shape[0]
    high = lax.Precision.HIGHEST
    for layer in range(LAYERS):
        padded = jnp.pad(hidden.astype(jnp.float32), ((DMAX, DMAX), (0, 0)))
        acc = jnp.zeros((length, WIDTH), jnp.float32)
        for tap in range(3):
            start = (DMAX + (tap - 1) * dilations[layer]).astype(jnp.int32)
            piece = lax.dynamic_slice_in_dim(padded, start, length, 0)
            acc = acc + jnp.dot(piece, conv_weight[layer, tap].astype(jnp.float32), precision=high)
        hidden = (hidden.astype(jnp.float32) + jax.nn.silu(acc + conv_bias[layer][None, :])).astype(jnp.bfloat16)
    hidden_wide = hidden.astype(jnp.float32)
    head = jnp.dot(hidden_wide, head_weight.astype(jnp.float32), precision=high).T
    obs = head[:STATE]
    logp = head[STATE:]
    first = (jnp.arange(length, dtype=jnp.int32) == 0)[None, :]
    elems = elements(obs, logp, params, present.astype(jnp.float32)[None, :], keep[None, :], first)
    result = doubling_prefix(elems, 1)
    grad = jnp.dot(hidden_wide.T, cotangent.astype(jnp.float32), precision=high)
    return result[1], grad


def reference(frames, conv_weight, conv_bias, dilations, head_weight, present, frame_keep, channel_params, head_cotangent):
    means = []
    grad_total = jnp.zeros((WIDTH, 2 * STATE), jnp.float32)
    for index in range(frames.shape[0]):
        mean_one, grad_one = one_take(frames[index], present[index], frame_keep[index], head_cotangent[index], conv_weight, conv_bias, dilations, head_weight, channel_params)
        means.append(mean_one)
        grad_total = grad_total + grad_one
    return jnp.stack(means), grad_total
```

```python
import jax
import jax.numpy as jnp
from jax import lax
from jax.sharding import PartitionSpec as P

STATE = 64
LAYERS = 3
DMAX = 64


def extended_2(block, sides, width):
    for axis, dim in sides:
        count = lax.axis_size(axis)
        forward = [(i, i + 1) for i in range(count - 1)]
        backward = [(target, source) for source, target in forward]
        low = lax.ppermute(
            lax.slice_in_dim(block, block.shape[dim] - width, None, axis=dim), axis, forward
        )
        high = lax.ppermute(lax.slice_in_dim(block, 0, width, axis=dim), axis, backward)
        block = jnp.concatenate([low, block, high], axis=dim)
    return block


def prefix_2(part, axis, combine, identity):
    place = lax.axis_index(axis)
    gathered = jax.tree.map(lambda a: lax.all_gather(a, axis), part)
    state = jax.tree.map(lambda a, e: jnp.zeros_like(a) + jnp.asarray(e, a.dtype), part, identity)

    def one(turn, state):
        return combine(
            state, jax.tree.map(lambda a: lax.dynamic_index_in_dim(a, turn, 0, False), gathered)
        )

    return lax.fori_loop(0, place, one, state)


def combine(early, late):
    a_one, b_one, c_one, e_one, j_one = early
    a_two, b_two, c_two, e_two, j_two = late
    denom = 1.0 + c_one * j_two
    new_a = a_two * a_one / denom
    new_b = a_two * (b_one + c_one * e_two) / denom + b_two
    new_c = a_two * a_two * c_one / denom + c_two
    new_e = a_one * (e_two - j_two * b_one) / denom + e_one
    new_j = a_one * a_one * j_two / denom + j_one
    return (new_a, new_b, new_c, new_e, new_j)


def doubling_prefix(elems, axis):
    length = elems[0].shape[axis]
    result = elems
    offset = 1
    while offset < length:
        moved = []
        for index, item in enumerate(result):
            fill_value = 1.0 if index == 0 else 0.0
            pad_shape = list(item.shape)
            pad_shape[axis] = offset
            fill = jnp.full(pad_shape, fill_value, item.dtype)
            kept = lax.slice_in_dim(item, 0, length - offset, axis=axis)
            moved.append(jnp.concatenate([fill, kept], axis=axis))
        result = combine(tuple(moved), result)
        offset = offset * 2
    return result


def exclusive_in_group(totals, axis):
    place = lax.axis_index(axis)
    gathered = lax.all_gather(totals, axis)
    inclusive = doubling_prefix(tuple(gathered[:, k] for k in range(5)), 0)
    inclusive = jnp.stack(inclusive, axis=1)
    earlier = lax.dynamic_index_in_dim(inclusive, jnp.maximum(place - 1, 0), 0, False)
    identity = jnp.zeros_like(earlier).at[0].set(1.0)
    earlier = jnp.where(place > 0, earlier, identity)
    return earlier, inclusive[-1]


def block_prefix(totals):
    inner_excl, group_total = exclusive_in_group(totals, "inner")
    outer_excl, _ = exclusive_in_group(group_total, "outer")
    return combine(tuple(outer_excl), tuple(inner_excl))


def elements(obs, logp, params, present, keep, first):
    rate = params[0][:, None]
    noise = params[1][:, None]
    scale = params[2][:, None]
    trans = jnp.exp(-rate) * keep
    prec = present * scale * jax.nn.softplus(logp)
    denom = 1.0 + noise * prec
    zeros = jnp.zeros_like(obs)
    elem_a = jnp.where(first, zeros, trans / denom)
    elem_b = jnp.where(first, prec * obs / (1.0 + prec), noise * prec * obs / denom)
    elem_c = jnp.where(first, 1.0 / (1.0 + prec), noise / denom)
    elem_e = jnp.where(first, zeros, trans * prec * obs / denom)
    elem_j = jnp.where(first, zeros, trans * trans * prec / denom)
    return (elem_a, elem_b, elem_c, elem_e, elem_j)


def conv_layer(extended, weights, bias, dilation):
    out_len = extended.shape[1] - 2 * DMAX
    acc = jnp.zeros((extended.shape[0], out_len, extended.shape[2]), jnp.float32)
    for tap in range(3):
        piece = lax.dynamic_slice_in_dim(extended, DMAX + (tap - 1) * dilation, out_len, 1)
        acc = acc + jnp.einsum(
            "tfw,wv->tfv", piece, weights[tap], preferred_element_type=jnp.float32
        )
    center = extended[:, DMAX : DMAX + out_len]
    return (center.astype(jnp.float32) + jax.nn.silu(acc + bias[None, None, :])).astype(
        jnp.bfloat16
    )


def per_device(
    frames,
    conv_weight,
    conv_bias,
    dilations,
    head_weight,
    present,
    frame_keep,
    channel_params,
    head_cotangent,
):
    block_len = frames.shape[1]
    position = lax.axis_index(("outer", "inner"))
    hidden = frames
    for layer in range(LAYERS):
        extended = extended_2(hidden, ((("outer", "inner"), 1),), DMAX)
        hidden = conv_layer(extended, conv_weight[layer], conv_bias[layer], dilations[layer])
    head = jnp.einsum("tfw,ws->tsf", hidden, head_weight, preferred_element_type=jnp.float32)
    obs = head[:, :STATE]
    logp = head[:, STATE:]
    places = position * block_len + jnp.arange(block_len, dtype=jnp.int32)
    first = (places == 0)[None, None, :]
    elems = elements(
        obs,
        logp,
        channel_params,
        present.astype(jnp.float32)[:, None, :],
        frame_keep[:, None, :],
        first,
    )
    local = doubling_prefix(elems, 2)
    totals = jnp.stack([item[:, :, -1] for item in local])
    prefix = block_prefix(totals)
    final = combine(tuple((item[:, :, None] for item in prefix)), local)
    grad_local = jnp.einsum(
        "tfw,tfs->ws", hidden, head_cotangent, preferred_element_type=jnp.float32
    )
    head_grad = lax.psum(grad_local, "inner")
    head_grad = lax.psum(head_grad, "outer")
    head_grad = lax.psum(head_grad, "take")
    return (final[1], head_grad)


def solution(mesh):
    return jax.shard_map(
        per_device,
        mesh=mesh,
        in_specs=(
            P("take", ("outer", "inner"), None),
            P(),
            P(),
            P(),
            P(),
            P("take", ("outer", "inner")),
            P("take", ("outer", "inner")),
            P(),
            P("take", ("outer", "inner"), None),
        ),
        out_specs=(P("take", None, ("outer", "inner")), P()),
        check_vma=False,
    )
```

```python
import jax
import jax.numpy as jnp
from jax import lax
from jax.sharding import PartitionSpec as P

STATE = 64
LAYERS = 3
DMAX = 64


def extended_2(block, sides, width):
    for axis, dim in sides:
        count = lax.axis_size(axis)
        forward = [(i, i + 1) for i in range(count - 1)]
        backward = [(target, source) for source, target in forward]
        low = lax.ppermute(
            lax.slice_in_dim(block, block.shape[dim] - width, None, axis=dim), axis, forward
        )
        high = lax.ppermute(lax.slice_in_dim(block, 0, width, axis=dim), axis, backward)
        block = jnp.concatenate([low, block, high], axis=dim)
    return block


def prefix_2(part, axis, combine, identity):
    place = lax.axis_index(axis)
    gathered = jax.tree.map(lambda a: lax.all_gather(a, axis), part)
    state = jax.tree.map(lambda a, e: jnp.zeros_like(a) + jnp.asarray(e, a.dtype), part, identity)

    def one(turn, state):
        return combine(
            state, jax.tree.map(lambda a: lax.dynamic_index_in_dim(a, turn, 0, False), gathered)
        )

    return lax.fori_loop(0, place, one, state)


def combine(early, late):
    a_one, b_one, c_one, e_one, j_one = early
    a_two, b_two, c_two, e_two, j_two = late
    denom = 1.0 + c_one * j_two
    new_a = a_two * a_one / denom
    new_b = a_two * (b_one + c_one * e_two) / denom + b_two
    new_c = a_two * a_two * c_one / denom + c_two
    new_e = a_one * (e_two - j_two * b_one) / denom + e_one
    new_j = a_one * a_one * j_two / denom + j_one
    return (new_a, new_b, new_c, new_e, new_j)


def doubling_prefix(elems, axis):
    length = elems[0].shape[axis]
    result = elems
    offset = 1
    while offset < length:
        moved = []
        for index, item in enumerate(result):
            fill_value = 1.0 if index == 0 else 0.0
            pad_shape = list(item.shape)
            pad_shape[axis] = offset
            fill = jnp.full(pad_shape, fill_value, item.dtype)
            kept = lax.slice_in_dim(item, 0, length - offset, axis=axis)
            moved.append(jnp.concatenate([fill, kept], axis=axis))
        result = combine(tuple(moved), result)
        offset = offset * 2
    return result


def butterfly_sum(value, axis):
    count = lax.axis_size(axis)
    step = 1
    while step < count:
        pairs = [(i, i ^ step) for i in range(count)]
        value = value + lax.ppermute(value, axis, pairs)
        step = step * 2
    return value


def block_prefix(totals, axis):
    count = lax.axis_size(axis)
    place = lax.axis_index(axis)
    identity = jnp.zeros_like(totals).at[0].set(1.0)

    def shifted(value, step):
        pairs = [(i, i + step) for i in range(count - step)]
        return lax.ppermute(value, axis, pairs)

    running = jnp.where(place >= 1, shifted(totals, 1), identity)
    step = 1
    while step < count:
        early = shifted(running, step)
        joined = jnp.stack(combine(tuple(early), tuple(running)))
        running = jnp.where(place >= step, joined, running)
        step = step * 2
    return running

def elements(obs, logp, params, present, keep, first):
    rate = params[0][:, None]
    noise = params[1][:, None]
    scale = params[2][:, None]
    trans = jnp.exp(-rate) * keep
    prec = present * scale * jax.nn.softplus(logp)
    denom = 1.0 + noise * prec
    zeros = jnp.zeros_like(obs)
    elem_a = jnp.where(first, zeros, trans / denom)
    elem_b = jnp.where(first, prec * obs / (1.0 + prec), noise * prec * obs / denom)
    elem_c = jnp.where(first, 1.0 / (1.0 + prec), noise / denom)
    elem_e = jnp.where(first, zeros, trans * prec * obs / denom)
    elem_j = jnp.where(first, zeros, trans * trans * prec / denom)
    return (elem_a, elem_b, elem_c, elem_e, elem_j)


def conv_layer(extended, weights, bias, dilation):
    out_len = extended.shape[1] - 2 * DMAX
    acc = jnp.zeros((extended.shape[0], out_len, extended.shape[2]), jnp.float32)
    for tap in range(3):
        piece = lax.dynamic_slice_in_dim(extended, DMAX + (tap - 1) * dilation, out_len, 1)
        acc = acc + jnp.einsum(
            "tfw,wv->tfv", piece, weights[tap], preferred_element_type=jnp.float32
        )
    center = extended[:, DMAX : DMAX + out_len]
    return (center.astype(jnp.float32) + jax.nn.silu(acc + bias[None, None, :])).astype(
        jnp.bfloat16
    )


def per_device(
    frames,
    conv_weight,
    conv_bias,
    dilations,
    head_weight,
    present,
    frame_keep,
    channel_params,
    head_cotangent,
):
    block_len = frames.shape[1]
    position = lax.axis_index(("outer", "inner"))
    hidden = frames
    for layer in range(LAYERS):
        extended = extended_2(hidden, ((("outer", "inner"), 1),), DMAX)
        hidden = conv_layer(extended, conv_weight[layer], conv_bias[layer], dilations[layer])
    head = jnp.einsum("tfw,ws->tsf", hidden, head_weight, preferred_element_type=jnp.float32)
    obs = head[:, :STATE]
    logp = head[:, STATE:]
    places = position * block_len + jnp.arange(block_len, dtype=jnp.int32)
    first = (places == 0)[None, None, :]
    elems = elements(
        obs,
        logp,
        channel_params,
        present.astype(jnp.float32)[:, None, :],
        frame_keep[:, None, :],
        first,
    )
    local = doubling_prefix(elems, 2)
    totals = jnp.stack([item[:, :, -1] for item in local])
    prefix = block_prefix(totals, ("outer", "inner"))
    final = combine(tuple((item[:, :, None] for item in prefix)), local)
    grad_local = jnp.einsum(
        "tfw,tfs->ws", hidden, head_cotangent, preferred_element_type=jnp.float32
    )
    head_grad = butterfly_sum(grad_local, "inner")
    head_grad = butterfly_sum(head_grad, "outer")
    head_grad = butterfly_sum(head_grad, "take")
    return (final[1], head_grad)


def solution(mesh):
    return jax.shard_map(
        per_device,
        mesh=mesh,
        in_specs=(
            P("take", ("outer", "inner"), None),
            P(),
            P(),
            P(),
            P(),
            P("take", ("outer", "inner")),
            P("take", ("outer", "inner")),
            P(),
            P("take", ("outer", "inner"), None),
        ),
        out_specs=(P("take", None, ("outer", "inner")), P()),
        check_vma=False,
    )
```

```python
import jax
import jax.numpy as jnp
from jax import lax
from jax.sharding import PartitionSpec as P

STATE = 64
LAYERS = 3
DMAX = 64


def extended_2(block, sides, width):
    for axis, dim in sides:
        count = lax.axis_size(axis)
        forward = [(i, i + 1) for i in range(count - 1)]
        backward = [(target, source) for source, target in forward]
        low = lax.ppermute(
            lax.slice_in_dim(block, block.shape[dim] - width, None, axis=dim), axis, forward
        )
        high = lax.ppermute(lax.slice_in_dim(block, 0, width, axis=dim), axis, backward)
        block = jnp.concatenate([low, block, high], axis=dim)
    return block


def prefix_2(part, axis, combine, identity):
    place = lax.axis_index(axis)
    gathered = jax.tree.map(lambda a: lax.all_gather(a, axis), part)
    state = jax.tree.map(lambda a, e: jnp.zeros_like(a) + jnp.asarray(e, a.dtype), part, identity)

    def one(turn, state):
        return combine(
            state, jax.tree.map(lambda a: lax.dynamic_index_in_dim(a, turn, 0, False), gathered)
        )

    return lax.fori_loop(0, place, one, state)


def combine(early, late):
    a_one, b_one, c_one, e_one, j_one = early
    a_two, b_two, c_two, e_two, j_two = late
    denom = 1.0 + c_one * j_two
    new_a = a_two * a_one / denom
    new_b = a_two * (b_one + c_one * e_two) / denom + b_two
    new_c = a_two * a_two * c_one / denom + c_two
    new_e = a_one * (e_two - j_two * b_one) / denom + e_one
    new_j = a_one * a_one * j_two / denom + j_one
    return (new_a, new_b, new_c, new_e, new_j)


def doubling_prefix(elems, axis):
    length = elems[0].shape[axis]
    result = elems
    offset = 1
    while offset < length:
        moved = []
        for index, item in enumerate(result):
            fill_value = 1.0 if index == 0 else 0.0
            pad_shape = list(item.shape)
            pad_shape[axis] = offset
            fill = jnp.full(pad_shape, fill_value, item.dtype)
            kept = lax.slice_in_dim(item, 0, length - offset, axis=axis)
            moved.append(jnp.concatenate([fill, kept], axis=axis))
        result = combine(tuple(moved), result)
        offset = offset * 2
    return result


def butterfly_sum(value, axis):
    count = lax.axis_size(axis)
    step = 1
    while step < count:
        pairs = [(i, i ^ step) for i in range(count)]
        value = value + lax.ppermute(value, axis, pairs)
        step = step * 2
    return value


def scan_and_sum(totals, grad, axes):
    prefix = jnp.zeros_like(totals).at[0].set(1.0)
    for axis in axes:
        count = lax.axis_size(axis)
        place = lax.axis_index(axis)
        step = 1
        while step < count:
            pairs = [(i, i ^ step) for i in range(count)]
            packed = jnp.concatenate([grad, totals.reshape(-1, grad.shape[1])])
            packed = lax.ppermute(packed, axis, pairs)
            other = packed[grad.shape[0] :].reshape(totals.shape)
            grad = grad + packed[: grad.shape[0]]
            lower = (place & step) != 0
            prefix = jnp.where(lower, jnp.stack(combine(tuple(other), tuple(prefix))), prefix)
            early = jnp.where(lower, other, totals)
            late = jnp.where(lower, totals, other)
            totals = jnp.stack(combine(tuple(early), tuple(late)))
            step = step * 2
    return prefix, grad

def elements(obs, logp, params, present, keep, first):
    rate = params[0][:, None]
    noise = params[1][:, None]
    scale = params[2][:, None]
    trans = jnp.exp(-rate) * keep
    prec = present * scale * jax.nn.softplus(logp)
    denom = 1.0 + noise * prec
    zeros = jnp.zeros_like(obs)
    elem_a = jnp.where(first, zeros, trans / denom)
    elem_b = jnp.where(first, prec * obs / (1.0 + prec), noise * prec * obs / denom)
    elem_c = jnp.where(first, 1.0 / (1.0 + prec), noise / denom)
    elem_e = jnp.where(first, zeros, trans * prec * obs / denom)
    elem_j = jnp.where(first, zeros, trans * trans * prec / denom)
    return (elem_a, elem_b, elem_c, elem_e, elem_j)


def conv_layer(extended, weights, bias, dilation):
    out_len = extended.shape[1] - 2 * DMAX
    acc = jnp.zeros((extended.shape[0], out_len, extended.shape[2]), jnp.float32)
    for tap in range(3):
        piece = lax.dynamic_slice_in_dim(extended, DMAX + (tap - 1) * dilation, out_len, 1)
        acc = acc + jnp.einsum(
            "tfw,wv->tfv", piece, weights[tap], preferred_element_type=jnp.float32
        )
    center = extended[:, DMAX : DMAX + out_len]
    return (center.astype(jnp.float32) + jax.nn.silu(acc + bias[None, None, :])).astype(
        jnp.bfloat16
    )


def per_device(
    frames,
    conv_weight,
    conv_bias,
    dilations,
    head_weight,
    present,
    frame_keep,
    channel_params,
    head_cotangent,
):
    block_len = frames.shape[1]
    position = lax.axis_index(("outer", "inner"))
    hidden = frames
    for layer in range(LAYERS):
        extended = extended_2(hidden, ((("outer", "inner"), 1),), DMAX)
        hidden = conv_layer(extended, conv_weight[layer], conv_bias[layer], dilations[layer])
    head = jnp.einsum("tfw,ws->tsf", hidden, head_weight, preferred_element_type=jnp.float32)
    obs = head[:, :STATE]
    logp = head[:, STATE:]
    places = position * block_len + jnp.arange(block_len, dtype=jnp.int32)
    first = (places == 0)[None, None, :]
    elems = elements(
        obs,
        logp,
        channel_params,
        present.astype(jnp.float32)[:, None, :],
        frame_keep[:, None, :],
        first,
    )
    grad_local = jnp.einsum(
        "tfw,tfs->ws", hidden, head_cotangent, preferred_element_type=jnp.float32
    )
    grad_local = butterfly_sum(grad_local, "take")
    local = doubling_prefix(elems, 2)
    totals = jnp.stack([item[:, :, -1] for item in local])
    prefix, head_grad = scan_and_sum(totals, grad_local, ("inner", "outer"))
    final = combine(tuple((item[:, :, None] for item in prefix)), local)
    return (final[1], head_grad)


def solution(mesh):
    return jax.shard_map(
        per_device,
        mesh=mesh,
        in_specs=(
            P("take", ("outer", "inner"), None),
            P(),
            P(),
            P(),
            P(),
            P("take", ("outer", "inner")),
            P("take", ("outer", "inner")),
            P(),
            P("take", ("outer", "inner"), None),
        ),
        out_specs=(P("take", None, ("outer", "inner")), P()),
        check_vma=False,
    )
```

```python
import jax
import jax.numpy as jnp
from jax import lax
from jax.sharding import PartitionSpec as P

STATE = 64
LAYERS = 3
DMAX = 64
HALO = 136


def extended_2(block, sides, width):
    for axis, dim in sides:
        count = lax.axis_size(axis)
        forward = [(i, i + 1) for i in range(count - 1)]
        backward = [(target, source) for source, target in forward]
        low = lax.ppermute(
            lax.slice_in_dim(block, block.shape[dim] - width, None, axis=dim), axis, forward
        )
        high = lax.ppermute(lax.slice_in_dim(block, 0, width, axis=dim), axis, backward)
        block = jnp.concatenate([low, block, high], axis=dim)
    return block


def prefix_2(part, axis, combine, identity):
    place = lax.axis_index(axis)
    gathered = jax.tree.map(lambda a: lax.all_gather(a, axis), part)
    state = jax.tree.map(lambda a, e: jnp.zeros_like(a) + jnp.asarray(e, a.dtype), part, identity)

    def one(turn, state):
        return combine(
            state, jax.tree.map(lambda a: lax.dynamic_index_in_dim(a, turn, 0, False), gathered)
        )

    return lax.fori_loop(0, place, one, state)


def combine(early, late):
    a_one, b_one, c_one, e_one, j_one = early
    a_two, b_two, c_two, e_two, j_two = late
    denom = 1.0 + c_one * j_two
    new_a = a_two * a_one / denom
    new_b = a_two * (b_one + c_one * e_two) / denom + b_two
    new_c = a_two * a_two * c_one / denom + c_two
    new_e = a_one * (e_two - j_two * b_one) / denom + e_one
    new_j = a_one * a_one * j_two / denom + j_one
    return (new_a, new_b, new_c, new_e, new_j)


def doubling_prefix(elems, axis):
    length = elems[0].shape[axis]
    result = elems
    offset = 1
    while offset < length:
        moved = []
        for index, item in enumerate(result):
            fill_value = 1.0 if index == 0 else 0.0
            pad_shape = list(item.shape)
            pad_shape[axis] = offset
            fill = jnp.full(pad_shape, fill_value, item.dtype)
            kept = lax.slice_in_dim(item, 0, length - offset, axis=axis)
            moved.append(jnp.concatenate([fill, kept], axis=axis))
        result = combine(tuple(moved), result)
        offset = offset * 2
    return result


def butterfly_sum(value, axis):
    count = lax.axis_size(axis)
    step = 1
    while step < count:
        pairs = [(i, i ^ step) for i in range(count)]
        value = value + lax.ppermute(value, axis, pairs)
        step = step * 2
    return value


def scan_and_sum(totals, grad, axes):
    prefix = jnp.zeros_like(totals).at[0].set(1.0)
    for axis in axes:
        count = lax.axis_size(axis)
        place = lax.axis_index(axis)
        step = 1
        while step < count:
            pairs = [(i, i ^ step) for i in range(count)]
            packed = jnp.concatenate([grad, totals.reshape(-1, grad.shape[1])])
            packed = lax.ppermute(packed, axis, pairs)
            other = packed[grad.shape[0] :].reshape(totals.shape)
            grad = grad + packed[: grad.shape[0]]
            lower = (place & step) != 0
            prefix = jnp.where(lower, jnp.stack(combine(tuple(other), tuple(prefix))), prefix)
            early = jnp.where(lower, other, totals)
            late = jnp.where(lower, totals, other)
            totals = jnp.stack(combine(tuple(early), tuple(late)))
            step = step * 2
    return prefix, grad

def elements(obs, logp, params, present, keep, first):
    rate = params[0][:, None]
    noise = params[1][:, None]
    scale = params[2][:, None]
    trans = jnp.exp(-rate) * keep
    prec = present * scale * jax.nn.softplus(logp)
    denom = 1.0 + noise * prec
    zeros = jnp.zeros_like(obs)
    elem_a = jnp.where(first, zeros, trans / denom)
    elem_b = jnp.where(first, prec * obs / (1.0 + prec), noise * prec * obs / denom)
    elem_c = jnp.where(first, 1.0 / (1.0 + prec), noise / denom)
    elem_e = jnp.where(first, zeros, trans * prec * obs / denom)
    elem_j = jnp.where(first, zeros, trans * trans * prec / denom)
    return (elem_a, elem_b, elem_c, elem_e, elem_j)


def conv_layer(extended, weights, bias, dilation):
    out_len = extended.shape[1] - 2 * DMAX
    acc = jnp.zeros((extended.shape[0], out_len, extended.shape[2]), jnp.float32)
    for tap in range(3):
        piece = lax.dynamic_slice_in_dim(extended, DMAX + (tap - 1) * dilation, out_len, 1)
        acc = acc + jnp.einsum(
            "tfw,wv->tfv", piece, weights[tap], preferred_element_type=jnp.float32
        )
    center = extended[:, DMAX : DMAX + out_len]
    return (center.astype(jnp.float32) + jax.nn.silu(acc + bias[None, None, :])).astype(
        jnp.bfloat16
    )


def per_device(
    frames,
    conv_weight,
    conv_bias,
    dilations,
    head_weight,
    present,
    frame_keep,
    channel_params,
    head_cotangent,
):
    block_len = frames.shape[1]
    position = lax.axis_index(("outer", "inner"))
    hidden = frames
    halo = HALO
    hidden = extended_2(hidden, ((("outer", "inner"), 1),), halo)
    count = lax.axis_size(("outer", "inner"))
    spots = position * block_len - halo + jnp.arange(block_len + 2 * halo, dtype=jnp.int32)
    inside = ((spots >= 0) & (spots < count * block_len))[None, :, None]
    pad = ((0, 0), (DMAX, DMAX), (0, 0))
    for layer in range(LAYERS):
        extended = jnp.pad(hidden, pad)
        hidden = conv_layer(extended, conv_weight[layer], conv_bias[layer], dilations[layer])
        hidden = jnp.where(inside, hidden, jnp.zeros_like(hidden))
    hidden = hidden[:, halo : halo + block_len]
    head = jnp.einsum("tfw,ws->tsf", hidden, head_weight, preferred_element_type=jnp.float32)
    obs = head[:, :STATE]
    logp = head[:, STATE:]
    places = position * block_len + jnp.arange(block_len, dtype=jnp.int32)
    first = (places == 0)[None, None, :]
    elems = elements(
        obs,
        logp,
        channel_params,
        present.astype(jnp.float32)[:, None, :],
        frame_keep[:, None, :],
        first,
    )
    grad_local = jnp.einsum(
        "tfw,tfs->ws", hidden, head_cotangent, preferred_element_type=jnp.float32
    )
    grad_local = butterfly_sum(grad_local, "take")
    local = doubling_prefix(elems, 2)
    totals = jnp.stack([item[:, :, -1] for item in local])
    prefix, head_grad = scan_and_sum(totals, grad_local, ("inner", "outer"))
    final = combine(tuple((item[:, :, None] for item in prefix)), local)
    return (final[1], head_grad)


def solution(mesh):
    return jax.shard_map(
        per_device,
        mesh=mesh,
        in_specs=(
            P("take", ("outer", "inner"), None),
            P(),
            P(),
            P(),
            P(),
            P("take", ("outer", "inner")),
            P("take", ("outer", "inner")),
            P(),
            P("take", ("outer", "inner"), None),
        ),
        out_specs=(P("take", None, ("outer", "inner")), P()),
        check_vma=False,
    )
```

```python
import jax
import jax.numpy as jnp
from jax import lax
from jax.sharding import PartitionSpec as P

STATE = 64
LAYERS = 3
DMAX = 64
HALO = 136


def extended_2(block, sides, width):
    for axis, dim in sides:
        count = lax.axis_size(axis)
        forward = [(i, i + 1) for i in range(count - 1)]
        backward = [(target, source) for source, target in forward]
        low = lax.ppermute(
            lax.slice_in_dim(block, block.shape[dim] - width, None, axis=dim), axis, forward
        )
        high = lax.ppermute(lax.slice_in_dim(block, 0, width, axis=dim), axis, backward)
        block = jnp.concatenate([low, block, high], axis=dim)
    return block


def prefix_2(part, axis, combine, identity):
    place = lax.axis_index(axis)
    gathered = jax.tree.map(lambda a: lax.all_gather(a, axis), part)
    state = jax.tree.map(lambda a, e: jnp.zeros_like(a) + jnp.asarray(e, a.dtype), part, identity)

    def one(turn, state):
        return combine(
            state, jax.tree.map(lambda a: lax.dynamic_index_in_dim(a, turn, 0, False), gathered)
        )

    return lax.fori_loop(0, place, one, state)


def combine(early, late):
    a_one, b_one, c_one, e_one, j_one = early
    a_two, b_two, c_two, e_two, j_two = late
    denom = 1.0 + c_one * j_two
    new_a = a_two * a_one / denom
    new_b = a_two * (b_one + c_one * e_two) / denom + b_two
    new_c = a_two * a_two * c_one / denom + c_two
    new_e = a_one * (e_two - j_two * b_one) / denom + e_one
    new_j = a_one * a_one * j_two / denom + j_one
    return (new_a, new_b, new_c, new_e, new_j)


def doubling_prefix(elems, axis):
    length = elems[0].shape[axis]
    result = elems
    offset = 1
    while offset < length:
        moved = []
        for index, item in enumerate(result):
            fill_value = 1.0 if index == 0 else 0.0
            pad_shape = list(item.shape)
            pad_shape[axis] = offset
            fill = jnp.full(pad_shape, fill_value, item.dtype)
            kept = lax.slice_in_dim(item, 0, length - offset, axis=axis)
            moved.append(jnp.concatenate([fill, kept], axis=axis))
        result = combine(tuple(moved), result)
        offset = offset * 2
    return result


def radices(count):
    sizes = []
    while count > 1:
        size = 2 if count % 4 else 4
        sizes.append(size)
        count = count // size
    if len(sizes) > 1 and sizes[-1] == 2:
        sizes = sizes[-1:] + sizes[:-1]
    return sizes


def digit_round(own, axis, radix, step):
    count = lax.axis_size(axis)
    digit = (lax.axis_index(axis) // step) % radix
    received = [
        lax.ppermute(own, axis, [(i, i ^ (k * step)) for i in range(count)])
        for k in range(1, radix)
    ]
    slots = []
    for j in range(radix):
        value = own
        for k in range(1, radix):
            value = jnp.where(digit == (j ^ k), received[k - 1], value)
        slots.append(value)
    return digit, slots


def group_sum(value, axis):
    step = 1
    for radix in radices(lax.axis_size(axis)):
        _, slots = digit_round(value, axis, radix, step)
        value = slots[0]
        for item in slots[1:]:
            value = value + item
        step = step * radix
    return value


def scan_and_sum(totals, grad, axes):
    prefix = jnp.zeros_like(totals).at[0].set(1.0)
    rows = grad.shape[0]
    for axis in axes:
        step = 1
        for radix in radices(lax.axis_size(axis)):
            packed = jnp.concatenate([grad, totals.reshape(-1, grad.shape[1])])
            digit, slots = digit_round(packed, axis, radix, step)
            grad = slots[0][:rows]
            for item in slots[1:]:
                grad = grad + item[:rows]
            parts = [item[rows:].reshape(totals.shape) for item in slots]
            earlier = [jnp.zeros_like(totals).at[0].set(1.0)]
            running = parts[0]
            for item in parts[1:]:
                earlier.append(running)
                running = jnp.stack(combine(tuple(running), tuple(item)))
            totals = running
            chosen = earlier[0]
            for j in range(1, radix):
                chosen = jnp.where(digit == j, earlier[j], chosen)
            prefix = jnp.stack(combine(tuple(chosen), tuple(prefix)))
            step = step * radix
    return prefix, grad

def elements(obs, logp, params, present, keep, first):
    rate = params[0][:, None]
    noise = params[1][:, None]
    scale = params[2][:, None]
    trans = jnp.exp(-rate) * keep
    prec = present * scale * jax.nn.softplus(logp)
    denom = 1.0 + noise * prec
    zeros = jnp.zeros_like(obs)
    elem_a = jnp.where(first, zeros, trans / denom)
    elem_b = jnp.where(first, prec * obs / (1.0 + prec), noise * prec * obs / denom)
    elem_c = jnp.where(first, 1.0 / (1.0 + prec), noise / denom)
    elem_e = jnp.where(first, zeros, trans * prec * obs / denom)
    elem_j = jnp.where(first, zeros, trans * trans * prec / denom)
    return (elem_a, elem_b, elem_c, elem_e, elem_j)


def conv_layer(extended, weights, bias, dilation):
    out_len = extended.shape[1] - 2 * DMAX
    acc = jnp.zeros((extended.shape[0], out_len, extended.shape[2]), jnp.float32)
    for tap in range(3):
        piece = lax.dynamic_slice_in_dim(extended, DMAX + (tap - 1) * dilation, out_len, 1)
        acc = acc + jnp.einsum(
            "tfw,wv->tfv", piece, weights[tap], preferred_element_type=jnp.float32
        )
    center = extended[:, DMAX : DMAX + out_len]
    return (center.astype(jnp.float32) + jax.nn.silu(acc + bias[None, None, :])).astype(
        jnp.bfloat16
    )


def per_device(
    frames,
    conv_weight,
    conv_bias,
    dilations,
    head_weight,
    present,
    frame_keep,
    channel_params,
    head_cotangent,
):
    block_len = frames.shape[1]
    position = lax.axis_index(("outer", "inner"))
    hidden = frames
    halo = HALO
    hidden = extended_2(hidden, ((("outer", "inner"), 1),), halo)
    count = lax.axis_size(("outer", "inner"))
    spots = position * block_len - halo + jnp.arange(block_len + 2 * halo, dtype=jnp.int32)
    inside = ((spots >= 0) & (spots < count * block_len))[None, :, None]
    pad = ((0, 0), (DMAX, DMAX), (0, 0))
    for layer in range(LAYERS):
        extended = jnp.pad(hidden, pad)
        hidden = conv_layer(extended, conv_weight[layer], conv_bias[layer], dilations[layer])
        hidden = jnp.where(inside, hidden, jnp.zeros_like(hidden))
    hidden = hidden[:, halo : halo + block_len]
    head = jnp.einsum("tfw,ws->tsf", hidden, head_weight, preferred_element_type=jnp.float32)
    obs = head[:, :STATE]
    logp = head[:, STATE:]
    places = position * block_len + jnp.arange(block_len, dtype=jnp.int32)
    first = (places == 0)[None, None, :]
    elems = elements(
        obs,
        logp,
        channel_params,
        present.astype(jnp.float32)[:, None, :],
        frame_keep[:, None, :],
        first,
    )
    grad_local = jnp.einsum(
        "tfw,tfs->ws", hidden, head_cotangent, preferred_element_type=jnp.float32
    )
    grad_local = group_sum(grad_local, "take")
    local = doubling_prefix(elems, 2)
    totals = jnp.stack([item[:, :, -1] for item in local])
    prefix, head_grad = scan_and_sum(totals, grad_local, ("inner", "outer"))
    final = combine(tuple((item[:, :, None] for item in prefix)), local)
    return (final[1], head_grad)


def solution(mesh):
    return jax.shard_map(
        per_device,
        mesh=mesh,
        in_specs=(
            P("take", ("outer", "inner"), None),
            P(),
            P(),
            P(),
            P(),
            P("take", ("outer", "inner")),
            P("take", ("outer", "inner")),
            P(),
            P("take", ("outer", "inner"), None),
        ),
        out_specs=(P("take", None, ("outer", "inner")), P()),
        check_vma=False,
    )
```

```python
import jax
import jax.numpy as jnp
from jax import lax
from jax.sharding import PartitionSpec as P

STATE = 64
LAYERS = 3
DMAX = 64
HALO = 136
TIME = ("high", "low", "x", "core")


def extended_2(block, sides, width):
    for axis, dim in sides:
        count = lax.axis_size(axis)
        forward = [(i, i + 1) for i in range(count - 1)]
        backward = [(target, source) for source, target in forward]
        low = lax.ppermute(
            lax.slice_in_dim(block, block.shape[dim] - width, None, axis=dim), axis, forward
        )
        high = lax.ppermute(lax.slice_in_dim(block, 0, width, axis=dim), axis, backward)
        block = jnp.concatenate([low, block, high], axis=dim)
    return block


def prefix_2(part, axis, combine, identity):
    place = lax.axis_index(axis)
    gathered = jax.tree.map(lambda a: lax.all_gather(a, axis), part)
    state = jax.tree.map(lambda a, e: jnp.zeros_like(a) + jnp.asarray(e, a.dtype), part, identity)

    def one(turn, state):
        return combine(
            state, jax.tree.map(lambda a: lax.dynamic_index_in_dim(a, turn, 0, False), gathered)
        )

    return lax.fori_loop(0, place, one, state)


def combine(early, late):
    a_one, b_one, c_one, e_one, j_one = early
    a_two, b_two, c_two, e_two, j_two = late
    denom = 1.0 + c_one * j_two
    new_a = a_two * a_one / denom
    new_b = a_two * (b_one + c_one * e_two) / denom + b_two
    new_c = a_two * a_two * c_one / denom + c_two
    new_e = a_one * (e_two - j_two * b_one) / denom + e_one
    new_j = a_one * a_one * j_two / denom + j_one
    return (new_a, new_b, new_c, new_e, new_j)


def doubling_prefix(elems, axis):
    length = elems[0].shape[axis]
    result = elems
    offset = 1
    while offset < length:
        moved = []
        for index, item in enumerate(result):
            fill_value = 1.0 if index == 0 else 0.0
            pad_shape = list(item.shape)
            pad_shape[axis] = offset
            fill = jnp.full(pad_shape, fill_value, item.dtype)
            kept = lax.slice_in_dim(item, 0, length - offset, axis=axis)
            moved.append(jnp.concatenate([fill, kept], axis=axis))
        result = combine(tuple(moved), result)
        offset = offset * 2
    return result


def gather_sum(value, axis):
    slots = lax.all_gather(value, axis)
    total = slots[0]
    for j in range(1, slots.shape[0]):
        total = total + slots[j]
    return total


def scan_and_sum(totals, grad, axes):
    prefix = jnp.zeros_like(totals).at[0].set(1.0)
    rows = grad.shape[0]
    for axis in axes:
        digit = lax.axis_index(axis)
        packed = jnp.concatenate([grad, totals.reshape(-1, grad.shape[1])])
        slots = lax.all_gather(packed, axis)
        radix = slots.shape[0]
        grad = slots[0, :rows]
        for j in range(1, radix):
            grad = grad + slots[j, :rows]
        parts = [slots[j, rows:].reshape(totals.shape) for j in range(radix)]
        earlier = [jnp.zeros_like(totals).at[0].set(1.0)]
        running = parts[0]
        for item in parts[1:]:
            earlier.append(running)
            running = jnp.stack(combine(tuple(running), tuple(item)))
        totals = running
        chosen = earlier[0]
        for j in range(1, radix):
            chosen = jnp.where(digit == j, earlier[j], chosen)
        prefix = jnp.stack(combine(tuple(chosen), tuple(prefix)))
    return prefix, grad

def elements(obs, logp, params, present, keep, first):
    rate = params[0][:, None]
    noise = params[1][:, None]
    scale = params[2][:, None]
    trans = jnp.exp(-rate) * keep
    prec = present * scale * jax.nn.softplus(logp)
    denom = 1.0 + noise * prec
    zeros = jnp.zeros_like(obs)
    elem_a = jnp.where(first, zeros, trans / denom)
    elem_b = jnp.where(first, prec * obs / (1.0 + prec), noise * prec * obs / denom)
    elem_c = jnp.where(first, 1.0 / (1.0 + prec), noise / denom)
    elem_e = jnp.where(first, zeros, trans * prec * obs / denom)
    elem_j = jnp.where(first, zeros, trans * trans * prec / denom)
    return (elem_a, elem_b, elem_c, elem_e, elem_j)


def conv_layer(extended, weights, bias, dilation):
    out_len = extended.shape[1] - 2 * DMAX
    acc = jnp.zeros((extended.shape[0], out_len, extended.shape[2]), jnp.float32)
    for tap in range(3):
        piece = lax.dynamic_slice_in_dim(extended, DMAX + (tap - 1) * dilation, out_len, 1)
        acc = acc + jnp.einsum(
            "tfw,wv->tfv", piece, weights[tap], preferred_element_type=jnp.float32
        )
    center = extended[:, DMAX : DMAX + out_len]
    return (center.astype(jnp.float32) + jax.nn.silu(acc + bias[None, None, :])).astype(
        jnp.bfloat16
    )


def per_device(
    frames,
    conv_weight,
    conv_bias,
    dilations,
    head_weight,
    present,
    frame_keep,
    channel_params,
    head_cotangent,
):
    block_len = frames.shape[1]
    position = lax.axis_index(TIME)
    hidden = frames
    halo = HALO
    hidden = extended_2(hidden, ((TIME, 1),), halo)
    count = lax.axis_size(TIME)
    spots = position * block_len - halo + jnp.arange(block_len + 2 * halo, dtype=jnp.int32)
    inside = ((spots >= 0) & (spots < count * block_len))[None, :, None]
    pad = ((0, 0), (DMAX, DMAX), (0, 0))
    for layer in range(LAYERS):
        extended = jnp.pad(hidden, pad)
        hidden = conv_layer(extended, conv_weight[layer], conv_bias[layer], dilations[layer])
        hidden = jnp.where(inside, hidden, jnp.zeros_like(hidden))
    hidden = hidden[:, halo : halo + block_len]
    head = jnp.einsum("tfw,ws->tsf", hidden, head_weight, preferred_element_type=jnp.float32)
    obs = head[:, :STATE]
    logp = head[:, STATE:]
    places = position * block_len + jnp.arange(block_len, dtype=jnp.int32)
    first = (places == 0)[None, None, :]
    elems = elements(
        obs,
        logp,
        channel_params,
        present.astype(jnp.float32)[:, None, :],
        frame_keep[:, None, :],
        first,
    )
    grad_local = jnp.einsum(
        "tfw,tfs->ws", hidden, head_cotangent, preferred_element_type=jnp.float32
    )
    grad_local = gather_sum(grad_local, "take")
    local = doubling_prefix(elems, 2)
    totals = jnp.stack([item[:, :, -1] for item in local])
    prefix, head_grad = scan_and_sum(totals, grad_local, ("core", "x", "low", "high"))
    final = combine(tuple((item[:, :, None] for item in prefix)), local)
    return (final[1], head_grad)


def solution(mesh):
    outer = mesh.shape["outer"]
    inner = mesh.shape["inner"]
    devices = mesh.devices.reshape(mesh.shape["take"], outer // 4, 4, inner // 2, 2)
    fine = jax.sharding.Mesh(devices, ("take",) + TIME)
    return jax.shard_map(
        per_device,
        mesh=fine,
        in_specs=(
            P("take", TIME, None),
            P(),
            P(),
            P(),
            P(),
            P("take", TIME),
            P("take", TIME),
            P(),
            P("take", TIME, None),
        ),
        out_specs=(P("take", None, TIME), P()),
        check_vma=False,
    )
```

```python
import jax
import jax.numpy as jnp
from jax import lax
from jax.sharding import PartitionSpec as P

STATE = 64
LAYERS = 3
DMAX = 64
HALO = 136
TIME = ("z3", "z2", "z1", "z0", "xh", "xl", "core")
TAKE = ("th", "tl")


def extended_2(block, sides, width):
    for axis, dim in sides:
        count = lax.axis_size(axis)
        forward = [(i, i + 1) for i in range(count - 1)]
        backward = [(target, source) for source, target in forward]
        low = lax.ppermute(
            lax.slice_in_dim(block, block.shape[dim] - width, None, axis=dim), axis, forward
        )
        high = lax.ppermute(lax.slice_in_dim(block, 0, width, axis=dim), axis, backward)
        block = jnp.concatenate([low, block, high], axis=dim)
    return block


def prefix_2(part, axis, combine, identity):
    place = lax.axis_index(axis)
    gathered = jax.tree.map(lambda a: lax.all_gather(a, axis), part)
    state = jax.tree.map(lambda a, e: jnp.zeros_like(a) + jnp.asarray(e, a.dtype), part, identity)

    def one(turn, state):
        return combine(
            state, jax.tree.map(lambda a: lax.dynamic_index_in_dim(a, turn, 0, False), gathered)
        )

    return lax.fori_loop(0, place, one, state)


def combine(early, late):
    a_one, b_one, c_one, e_one, j_one = early
    a_two, b_two, c_two, e_two, j_two = late
    denom = 1.0 + c_one * j_two
    new_a = a_two * a_one / denom
    new_b = a_two * (b_one + c_one * e_two) / denom + b_two
    new_c = a_two * a_two * c_one / denom + c_two
    new_e = a_one * (e_two - j_two * b_one) / denom + e_one
    new_j = a_one * a_one * j_two / denom + j_one
    return (new_a, new_b, new_c, new_e, new_j)


def doubling_prefix(elems, axis):
    length = elems[0].shape[axis]
    result = elems
    offset = 1
    while offset < length:
        moved = []
        for index, item in enumerate(result):
            fill_value = 1.0 if index == 0 else 0.0
            pad_shape = list(item.shape)
            pad_shape[axis] = offset
            fill = jnp.full(pad_shape, fill_value, item.dtype)
            kept = lax.slice_in_dim(item, 0, length - offset, axis=axis)
            moved.append(jnp.concatenate([fill, kept], axis=axis))
        result = combine(tuple(moved), result)
        offset = offset * 2
    return result


def gather_sum(value, axis):
    slots = lax.all_gather(value, axis)
    total = slots[0]
    for j in range(1, slots.shape[0]):
        total = total + slots[j]
    return total


def scan_and_sum(totals, grad, axes):
    prefix = jnp.zeros_like(totals).at[0].set(1.0)
    rows = grad.shape[0]
    for axis in axes:
        digit = lax.axis_index(axis)
        packed = jnp.concatenate([grad, totals.reshape(-1, grad.shape[1])])
        slots = lax.all_gather(packed, axis)
        radix = slots.shape[0]
        grad = slots[0, :rows]
        for j in range(1, radix):
            grad = grad + slots[j, :rows]
        parts = [slots[j, rows:].reshape(totals.shape) for j in range(radix)]
        earlier = [jnp.zeros_like(totals).at[0].set(1.0)]
        running = parts[0]
        for item in parts[1:]:
            earlier.append(running)
            running = jnp.stack(combine(tuple(running), tuple(item)))
        totals = running
        chosen = earlier[0]
        for j in range(1, radix):
            chosen = jnp.where(digit == j, earlier[j], chosen)
        prefix = jnp.stack(combine(tuple(chosen), tuple(prefix)))
    return prefix, grad

def elements(obs, logp, params, present, keep, first):
    rate = params[0][:, None]
    noise = params[1][:, None]
    scale = params[2][:, None]
    trans = jnp.exp(-rate) * keep
    prec = present * scale * jax.nn.softplus(logp)
    denom = 1.0 + noise * prec
    zeros = jnp.zeros_like(obs)
    elem_a = jnp.where(first, zeros, trans / denom)
    elem_b = jnp.where(first, prec * obs / (1.0 + prec), noise * prec * obs / denom)
    elem_c = jnp.where(first, 1.0 / (1.0 + prec), noise / denom)
    elem_e = jnp.where(first, zeros, trans * prec * obs / denom)
    elem_j = jnp.where(first, zeros, trans * trans * prec / denom)
    return (elem_a, elem_b, elem_c, elem_e, elem_j)


def conv_layer(extended, weights, bias, dilation):
    out_len = extended.shape[1] - 2 * DMAX
    acc = jnp.zeros((extended.shape[0], out_len, extended.shape[2]), jnp.float32)
    for tap in range(3):
        piece = lax.dynamic_slice_in_dim(extended, DMAX + (tap - 1) * dilation, out_len, 1)
        acc = acc + jnp.einsum(
            "tfw,wv->tfv", piece, weights[tap], preferred_element_type=jnp.float32
        )
    center = extended[:, DMAX : DMAX + out_len]
    return (center.astype(jnp.float32) + jax.nn.silu(acc + bias[None, None, :])).astype(
        jnp.bfloat16
    )


def per_device(
    frames,
    conv_weight,
    conv_bias,
    dilations,
    head_weight,
    present,
    frame_keep,
    channel_params,
    head_cotangent,
):
    block_len = frames.shape[1]
    position = lax.axis_index(TIME)
    hidden = frames
    halo = HALO
    hidden = extended_2(hidden, ((TIME, 1),), halo)
    count = lax.axis_size(TIME)
    spots = position * block_len - halo + jnp.arange(block_len + 2 * halo, dtype=jnp.int32)
    inside = ((spots >= 0) & (spots < count * block_len))[None, :, None]
    pad = ((0, 0), (DMAX, DMAX), (0, 0))
    for layer in range(LAYERS):
        extended = jnp.pad(hidden, pad)
        hidden = conv_layer(extended, conv_weight[layer], conv_bias[layer], dilations[layer])
        hidden = jnp.where(inside, hidden, jnp.zeros_like(hidden))
    hidden = hidden[:, halo : halo + block_len]
    head = jnp.einsum("tfw,ws->tsf", hidden, head_weight, preferred_element_type=jnp.float32)
    obs = head[:, :STATE]
    logp = head[:, STATE:]
    places = position * block_len + jnp.arange(block_len, dtype=jnp.int32)
    first = (places == 0)[None, None, :]
    elems = elements(
        obs,
        logp,
        channel_params,
        present.astype(jnp.float32)[:, None, :],
        frame_keep[:, None, :],
        first,
    )
    grad_local = jnp.einsum(
        "tfw,tfs->ws", hidden, head_cotangent, preferred_element_type=jnp.float32
    )
    grad_local = gather_sum(gather_sum(grad_local, "tl"), "th")
    local = doubling_prefix(elems, 2)
    totals = jnp.stack([item[:, :, -1] for item in local])
    prefix, head_grad = scan_and_sum(totals, grad_local, TIME[::-1])
    final = combine(tuple((item[:, :, None] for item in prefix)), local)
    return (final[1], head_grad)


def solution(mesh):
    devices = mesh.devices.reshape((2,) * (len(TAKE) + len(TIME)))
    fine = jax.sharding.Mesh(devices, TAKE + TIME)
    return jax.shard_map(
        per_device,
        mesh=fine,
        in_specs=(
            P(TAKE, TIME, None),
            P(),
            P(),
            P(),
            P(),
            P(TAKE, TIME),
            P(TAKE, TIME),
            P(),
            P(TAKE, TIME, None),
        ),
        out_specs=(P(TAKE, None, TIME), P()),
        check_vma=False,
    )
```

```python
import jax
import jax.numpy as jnp
from jax import lax
from jax.sharding import PartitionSpec as P

STATE = 64
LAYERS = 3
DMAX = 64
HALO = 136
TIME = ("z3", "z2", "z1", "z0", "xh", "xl", "core")
TAKE = ("th", "tl")


def extended_2(block, sides, width):
    for axis, dim in sides:
        count = lax.axis_size(axis)
        forward = [(i, i + 1) for i in range(count - 1)]
        backward = [(target, source) for source, target in forward]
        low = lax.ppermute(
            lax.slice_in_dim(block, block.shape[dim] - width, None, axis=dim), axis, forward
        )
        high = lax.ppermute(lax.slice_in_dim(block, 0, width, axis=dim), axis, backward)
        block = jnp.concatenate([low, block, high], axis=dim)
    return block


def prefix_2(part, axis, combine, identity):
    place = lax.axis_index(axis)
    gathered = jax.tree.map(lambda a: lax.all_gather(a, axis), part)
    state = jax.tree.map(lambda a, e: jnp.zeros_like(a) + jnp.asarray(e, a.dtype), part, identity)

    def one(turn, state):
        return combine(
            state, jax.tree.map(lambda a: lax.dynamic_index_in_dim(a, turn, 0, False), gathered)
        )

    return lax.fori_loop(0, place, one, state)


def combine(early, late):
    a_one, b_one, c_one, e_one, j_one = early
    a_two, b_two, c_two, e_two, j_two = late
    denom = 1.0 + c_one * j_two
    new_a = a_two * a_one / denom
    new_b = a_two * (b_one + c_one * e_two) / denom + b_two
    new_c = a_two * a_two * c_one / denom + c_two
    new_e = a_one * (e_two - j_two * b_one) / denom + e_one
    new_j = a_one * a_one * j_two / denom + j_one
    return (new_a, new_b, new_c, new_e, new_j)


def doubling_prefix(elems, axis):
    length = elems[0].shape[axis]
    result = elems
    offset = 1
    while offset < length:
        moved = []
        for index, item in enumerate(result):
            fill_value = 1.0 if index == 0 else 0.0
            pad_shape = list(item.shape)
            pad_shape[axis] = offset
            fill = jnp.full(pad_shape, fill_value, item.dtype)
            kept = lax.slice_in_dim(item, 0, length - offset, axis=axis)
            moved.append(jnp.concatenate([fill, kept], axis=axis))
        result = combine(tuple(moved), result)
        offset = offset * 2
    return result


def pair_sum(value, axis):
    return value + lax.ppermute(value, axis, [(0, 1), (1, 0)])


def gather_sum(value, axis):
    slots = lax.all_gather(value, axis)
    total = slots[0]
    for j in range(1, slots.shape[0]):
        total = total + slots[j]
    return total


def scan_and_sum(totals, grad, axes):
    prefix = jnp.zeros_like(totals).at[0].set(1.0)
    rows = grad.shape[0]
    for axis in axes:
        digit = lax.axis_index(axis)
        packed = jnp.concatenate([grad, totals.reshape(-1, grad.shape[1])])
        slots = lax.all_gather(packed, axis)
        radix = slots.shape[0]
        grad = slots[0, :rows]
        for j in range(1, radix):
            grad = grad + slots[j, :rows]
        parts = [slots[j, rows:].reshape(totals.shape) for j in range(radix)]
        earlier = [jnp.zeros_like(totals).at[0].set(1.0)]
        running = parts[0]
        for item in parts[1:]:
            earlier.append(running)
            running = jnp.stack(combine(tuple(running), tuple(item)))
        totals = running
        chosen = earlier[0]
        for j in range(1, radix):
            chosen = jnp.where(digit == j, earlier[j], chosen)
        prefix = jnp.stack(combine(tuple(chosen), tuple(prefix)))
    return prefix, grad

def elements(obs, logp, params, present, keep, first):
    rate = params[0][:, None]
    noise = params[1][:, None]
    scale = params[2][:, None]
    trans = jnp.exp(-rate) * keep
    prec = present * scale * jax.nn.softplus(logp)
    denom = 1.0 + noise * prec
    zeros = jnp.zeros_like(obs)
    elem_a = jnp.where(first, zeros, trans / denom)
    elem_b = jnp.where(first, prec * obs / (1.0 + prec), noise * prec * obs / denom)
    elem_c = jnp.where(first, 1.0 / (1.0 + prec), noise / denom)
    elem_e = jnp.where(first, zeros, trans * prec * obs / denom)
    elem_j = jnp.where(first, zeros, trans * trans * prec / denom)
    return (elem_a, elem_b, elem_c, elem_e, elem_j)


def conv_layer(extended, weights, bias, dilation):
    out_len = extended.shape[1] - 2 * DMAX
    acc = jnp.zeros((extended.shape[0], out_len, extended.shape[2]), jnp.float32)
    for tap in range(3):
        piece = lax.dynamic_slice_in_dim(extended, DMAX + (tap - 1) * dilation, out_len, 1)
        acc = acc + jnp.einsum(
            "tfw,wv->tfv", piece, weights[tap], preferred_element_type=jnp.float32
        )
    center = extended[:, DMAX : DMAX + out_len]
    return (center.astype(jnp.float32) + jax.nn.silu(acc + bias[None, None, :])).astype(
        jnp.bfloat16
    )


def per_device(
    frames,
    conv_weight,
    conv_bias,
    dilations,
    head_weight,
    present,
    frame_keep,
    channel_params,
    head_cotangent,
):
    block_len = frames.shape[1]
    position = lax.axis_index(TIME)
    hidden = frames
    halo = HALO
    hidden = extended_2(hidden, ((TIME, 1),), halo)
    count = lax.axis_size(TIME)
    spots = position * block_len - halo + jnp.arange(block_len + 2 * halo, dtype=jnp.int32)
    inside = ((spots >= 0) & (spots < count * block_len))[None, :, None]
    pad = ((0, 0), (DMAX, DMAX), (0, 0))
    for layer in range(LAYERS):
        extended = jnp.pad(hidden, pad)
        hidden = conv_layer(extended, conv_weight[layer], conv_bias[layer], dilations[layer])
        hidden = jnp.where(inside, hidden, jnp.zeros_like(hidden))
    hidden = hidden[:, halo : halo + block_len]
    head = jnp.einsum("tfw,ws->tsf", hidden, head_weight, preferred_element_type=jnp.float32)
    obs = head[:, :STATE]
    logp = head[:, STATE:]
    places = position * block_len + jnp.arange(block_len, dtype=jnp.int32)
    first = (places == 0)[None, None, :]
    elems = elements(
        obs,
        logp,
        channel_params,
        present.astype(jnp.float32)[:, None, :],
        frame_keep[:, None, :],
        first,
    )
    grad_local = jnp.einsum(
        "tfw,tfs->ws", hidden, head_cotangent, preferred_element_type=jnp.float32
    )
    grad_local = pair_sum(pair_sum(grad_local, "tl"), "th")
    local = doubling_prefix(elems, 2)
    totals = jnp.stack([item[:, :, -1] for item in local])
    prefix, head_grad = scan_and_sum(totals, grad_local, TIME[::-1])
    final = combine(tuple((item[:, :, None] for item in prefix)), local)
    return (final[1], head_grad)


def solution(mesh):
    devices = mesh.devices.reshape((2,) * (len(TAKE) + len(TIME)))
    fine = jax.sharding.Mesh(devices, TAKE + TIME)
    return jax.shard_map(
        per_device,
        mesh=fine,
        in_specs=(
            P(TAKE, TIME, None),
            P(),
            P(),
            P(),
            P(),
            P(TAKE, TIME),
            P(TAKE, TIME),
            P(),
            P(TAKE, TIME, None),
        ),
        out_specs=(P(TAKE, None, TIME), P()),
        check_vma=False,
    )
```

```python
import jax
import jax.numpy as jnp
from jax import lax
from jax.sharding import PartitionSpec as P

STATE = 64
LAYERS = 3
DMAX = 64
HALO = 136
TIME = ("z3", "z2", "z1", "z0", "xh", "xl", "core")
TAKE = ("th", "tl")


def extended_2(block, sides, width):
    for axis, dim in sides:
        count = lax.axis_size(axis)
        forward = [(i, i + 1) for i in range(count - 1)]
        backward = [(target, source) for source, target in forward]
        low = lax.ppermute(
            lax.slice_in_dim(block, block.shape[dim] - width, None, axis=dim), axis, forward
        )
        high = lax.ppermute(lax.slice_in_dim(block, 0, width, axis=dim), axis, backward)
        block = jnp.concatenate([low, block, high], axis=dim)
    return block


def prefix_2(part, axis, combine, identity):
    place = lax.axis_index(axis)
    gathered = jax.tree.map(lambda a: lax.all_gather(a, axis), part)
    state = jax.tree.map(lambda a, e: jnp.zeros_like(a) + jnp.asarray(e, a.dtype), part, identity)

    def one(turn, state):
        return combine(
            state, jax.tree.map(lambda a: lax.dynamic_index_in_dim(a, turn, 0, False), gathered)
        )

    return lax.fori_loop(0, place, one, state)


def combine(early, late):
    a_one, b_one, c_one, e_one, j_one = early
    a_two, b_two, c_two, e_two, j_two = late
    denom = 1.0 + c_one * j_two
    new_a = a_two * a_one / denom
    new_b = a_two * (b_one + c_one * e_two) / denom + b_two
    new_c = a_two * a_two * c_one / denom + c_two
    new_e = a_one * (e_two - j_two * b_one) / denom + e_one
    new_j = a_one * a_one * j_two / denom + j_one
    return (new_a, new_b, new_c, new_e, new_j)


def doubling_prefix(elems, axis):
    length = elems[0].shape[axis]
    result = elems
    offset = 1
    while offset < length:
        moved = []
        for index, item in enumerate(result):
            fill_value = 1.0 if index == 0 else 0.0
            pad_shape = list(item.shape)
            pad_shape[axis] = offset
            fill = jnp.full(pad_shape, fill_value, item.dtype)
            kept = lax.slice_in_dim(item, 0, length - offset, axis=axis)
            moved.append(jnp.concatenate([fill, kept], axis=axis))
        result = combine(tuple(moved), result)
        offset = offset * 2
    return result


def gather_sum(value, axis):
    slots = lax.all_gather(value, axis)
    total = slots[0]
    for j in range(1, slots.shape[0]):
        total = total + slots[j]
    return total


def scan_and_sum(totals, grad, axes):
    identity = (jnp.ones_like(totals[0]),) + tuple(jnp.zeros_like(item) for item in totals[1:])
    prefix = identity
    rows = grad.shape[0]
    width = totals[0].shape[0]
    for axis in axes:
        digit = lax.axis_index(axis)
        slots = lax.all_gather(jnp.concatenate((grad,) + tuple(totals)), axis)
        radix = slots.shape[0]
        grad = slots[0, :rows]
        for j in range(1, radix):
            grad = grad + slots[j, :rows]
        parts = [
            tuple(slots[j, rows + k * width : rows + (k + 1) * width] for k in range(len(totals)))
            for j in range(radix)
        ]
        earlier = [identity]
        running = parts[0]
        for item in parts[1:]:
            earlier.append(running)
            running = combine(running, item)
        totals = running
        chosen = earlier[0]
        for j in range(1, radix):
            chosen = tuple(jnp.where(digit == j, e, c) for e, c in zip(earlier[j], chosen))
        prefix = combine(chosen, prefix)
    return prefix, grad

def elements(obs, logp, params, present, keep, first):
    rate = params[0][:, None]
    noise = params[1][:, None]
    scale = params[2][:, None]
    trans = jnp.exp(-rate) * keep
    prec = present * scale * jax.nn.softplus(logp)
    denom = 1.0 + noise * prec
    zeros = jnp.zeros_like(obs)
    elem_a = jnp.where(first, zeros, trans / denom)
    elem_b = jnp.where(first, prec * obs / (1.0 + prec), noise * prec * obs / denom)
    elem_c = jnp.where(first, 1.0 / (1.0 + prec), noise / denom)
    elem_e = jnp.where(first, zeros, trans * prec * obs / denom)
    elem_j = jnp.where(first, zeros, trans * trans * prec / denom)
    return (elem_a, elem_b, elem_c, elem_e, elem_j)


def conv_layer(extended, weights, bias, dilation):
    out_len = extended.shape[1] - 2 * DMAX
    acc = jnp.zeros((extended.shape[0], out_len, extended.shape[2]), jnp.float32)
    for tap in range(3):
        piece = lax.dynamic_slice_in_dim(extended, DMAX + (tap - 1) * dilation, out_len, 1)
        acc = acc + jnp.einsum(
            "tfw,wv->tfv", piece, weights[tap], preferred_element_type=jnp.float32
        )
    center = extended[:, DMAX : DMAX + out_len]
    return (center.astype(jnp.float32) + jax.nn.silu(acc + bias[None, None, :])).astype(
        jnp.bfloat16
    )


def per_device(
    frames,
    conv_weight,
    conv_bias,
    dilations,
    head_weight,
    present,
    frame_keep,
    channel_params,
    head_cotangent,
):
    block_len = frames.shape[1]
    position = lax.axis_index(TIME)
    hidden = frames
    halo = HALO
    hidden = extended_2(hidden, ((TIME, 1),), halo)
    count = lax.axis_size(TIME)
    spots = position * block_len - halo + jnp.arange(block_len + 2 * halo, dtype=jnp.int32)
    inside = ((spots >= 0) & (spots < count * block_len))[None, :, None]
    pad = ((0, 0), (DMAX, DMAX), (0, 0))
    for layer in range(LAYERS):
        extended = jnp.pad(hidden, pad)
        hidden = conv_layer(extended, conv_weight[layer], conv_bias[layer], dilations[layer])
        hidden = jnp.where(inside, hidden, jnp.zeros_like(hidden))
    hidden = hidden[:, halo : halo + block_len]
    head = jnp.einsum("tfw,ws->tsf", hidden, head_weight, preferred_element_type=jnp.float32)
    obs = head[:, :STATE]
    logp = head[:, STATE:]
    places = position * block_len + jnp.arange(block_len, dtype=jnp.int32)
    first = (places == 0)[None, None, :]
    elems = elements(
        obs,
        logp,
        channel_params,
        present.astype(jnp.float32)[:, None, :],
        frame_keep[:, None, :],
        first,
    )
    grad_local = jnp.einsum(
        "tfw,tfs->ws", hidden, head_cotangent, preferred_element_type=jnp.float32
    )
    grad_local = gather_sum(gather_sum(grad_local, "tl"), "th")
    local = doubling_prefix(elems, 2)
    totals = tuple(item[:, :, -1].reshape(-1, grad_local.shape[1]) for item in local)
    prefix, head_grad = scan_and_sum(totals, grad_local, TIME[::-1])
    prefix = tuple(item.reshape(local[0].shape[:2])[:, :, None] for item in prefix)
    final = combine(prefix, local)
    return (final[1], head_grad)


def solution(mesh):
    devices = mesh.devices.reshape((2,) * (len(TAKE) + len(TIME)))
    fine = jax.sharding.Mesh(devices, TAKE + TIME)
    return jax.shard_map(
        per_device,
        mesh=fine,
        in_specs=(
            P(TAKE, TIME, None),
            P(),
            P(),
            P(),
            P(),
            P(TAKE, TIME),
            P(TAKE, TIME),
            P(),
            P(TAKE, TIME, None),
        ),
        out_specs=(P(TAKE, None, TIME), P()),
        check_vma=False,
    )
```

```python
import jax
import jax.numpy as jnp
from jax import lax
from jax.sharding import PartitionSpec as P

STATE = 64
LAYERS = 3
DMAX = 64
HALO = 136
TIME = ("z3", "z2", "z1", "z0", "xh", "xl", "core")
TAKE = ("th", "tl")
ROUNDS = ((("tl",), "core"), (("th",), "xl"), ((), "xh"), ((), "z0"), ((), "z1"), ((), "z2"), ((), "z3"))


def extended_2(block, sides, width):
    for axis, dim in sides:
        count = lax.axis_size(axis)
        forward = [(i, i + 1) for i in range(count - 1)]
        backward = [(target, source) for source, target in forward]
        low = lax.ppermute(
            lax.slice_in_dim(block, block.shape[dim] - width, None, axis=dim), axis, forward
        )
        high = lax.ppermute(lax.slice_in_dim(block, 0, width, axis=dim), axis, backward)
        block = jnp.concatenate([low, block, high], axis=dim)
    return block


def prefix_2(part, axis, combine, identity):
    place = lax.axis_index(axis)
    gathered = jax.tree.map(lambda a: lax.all_gather(a, axis), part)
    state = jax.tree.map(lambda a, e: jnp.zeros_like(a) + jnp.asarray(e, a.dtype), part, identity)

    def one(turn, state):
        return combine(
            state, jax.tree.map(lambda a: lax.dynamic_index_in_dim(a, turn, 0, False), gathered)
        )

    return lax.fori_loop(0, place, one, state)


def combine(early, late):
    a_one, b_one, c_one, e_one, j_one = early
    a_two, b_two, c_two, e_two, j_two = late
    denom = 1.0 + c_one * j_two
    new_a = a_two * a_one / denom
    new_b = a_two * (b_one + c_one * e_two) / denom + b_two
    new_c = a_two * a_two * c_one / denom + c_two
    new_e = a_one * (e_two - j_two * b_one) / denom + e_one
    new_j = a_one * a_one * j_two / denom + j_one
    return (new_a, new_b, new_c, new_e, new_j)


def doubling_prefix(elems, axis):
    length = elems[0].shape[axis]
    result = elems
    offset = 1
    while offset < length:
        moved = []
        for index, item in enumerate(result):
            fill_value = 1.0 if index == 0 else 0.0
            pad_shape = list(item.shape)
            pad_shape[axis] = offset
            fill = jnp.full(pad_shape, fill_value, item.dtype)
            kept = lax.slice_in_dim(item, 0, length - offset, axis=axis)
            moved.append(jnp.concatenate([fill, kept], axis=axis))
        result = combine(tuple(moved), result)
        offset = offset * 2
    return result


def gather_sum(value, axis):
    slots = lax.all_gather(value, axis)
    total = slots[0]
    for j in range(1, slots.shape[0]):
        total = total + slots[j]
    return total


def scan_and_sum(totals, grad, rounds):
    identity = (jnp.ones_like(totals[0]),) + tuple(jnp.zeros_like(item) for item in totals[1:])
    prefix = identity
    rows = grad.shape[0]
    width = totals[0].shape[0]
    for extra, axis in rounds:
        digit = lax.axis_index(axis)
        slots = lax.all_gather(jnp.concatenate((grad,) + tuple(totals)), extra + (axis,))
        grad = slots[0, :rows]
        for j in range(1, slots.shape[0]):
            grad = grad + slots[j, :rows]
        radix = lax.axis_size(axis)
        if extra:
            slots = slots.reshape((-1, radix) + slots.shape[1:])
            slots = lax.dynamic_index_in_dim(slots, lax.axis_index(extra), 0, False)
        parts = [
            tuple(slots[j, rows + k * width : rows + (k + 1) * width] for k in range(len(totals)))
            for j in range(radix)
        ]
        earlier = [identity]
        running = parts[0]
        for item in parts[1:]:
            earlier.append(running)
            running = combine(running, item)
        totals = running
        chosen = earlier[0]
        for j in range(1, radix):
            chosen = tuple(jnp.where(digit == j, e, c) for e, c in zip(earlier[j], chosen))
        prefix = combine(chosen, prefix)
    return prefix, grad

def elements(obs, logp, params, present, keep, first):
    rate = params[0][:, None]
    noise = params[1][:, None]
    scale = params[2][:, None]
    trans = jnp.exp(-rate) * keep
    prec = present * scale * jax.nn.softplus(logp)
    denom = 1.0 + noise * prec
    zeros = jnp.zeros_like(obs)
    elem_a = jnp.where(first, zeros, trans / denom)
    elem_b = jnp.where(first, prec * obs / (1.0 + prec), noise * prec * obs / denom)
    elem_c = jnp.where(first, 1.0 / (1.0 + prec), noise / denom)
    elem_e = jnp.where(first, zeros, trans * prec * obs / denom)
    elem_j = jnp.where(first, zeros, trans * trans * prec / denom)
    return (elem_a, elem_b, elem_c, elem_e, elem_j)


def conv_layer(extended, weights, bias, dilation):
    out_len = extended.shape[1] - 2 * DMAX
    acc = jnp.zeros((extended.shape[0], out_len, extended.shape[2]), jnp.float32)
    for tap in range(3):
        piece = lax.dynamic_slice_in_dim(extended, DMAX + (tap - 1) * dilation, out_len, 1)
        acc = acc + jnp.einsum(
            "tfw,wv->tfv", piece, weights[tap], preferred_element_type=jnp.float32
        )
    center = extended[:, DMAX : DMAX + out_len]
    return (center.astype(jnp.float32) + jax.nn.silu(acc + bias[None, None, :])).astype(
        jnp.bfloat16
    )


def per_device(
    frames,
    conv_weight,
    conv_bias,
    dilations,
    head_weight,
    present,
    frame_keep,
    channel_params,
    head_cotangent,
):
    block_len = frames.shape[1]
    position = lax.axis_index(TIME)
    hidden = frames
    halo = HALO
    hidden = extended_2(hidden, ((TIME, 1),), halo)
    count = lax.axis_size(TIME)
    spots = position * block_len - halo + jnp.arange(block_len + 2 * halo, dtype=jnp.int32)
    inside = ((spots >= 0) & (spots < count * block_len))[None, :, None]
    pad = ((0, 0), (DMAX, DMAX), (0, 0))
    for layer in range(LAYERS):
        extended = jnp.pad(hidden, pad)
        hidden = conv_layer(extended, conv_weight[layer], conv_bias[layer], dilations[layer])
        hidden = jnp.where(inside, hidden, jnp.zeros_like(hidden))
    hidden = hidden[:, halo : halo + block_len]
    head = jnp.einsum("tfw,ws->tsf", hidden, head_weight, preferred_element_type=jnp.float32)
    obs = head[:, :STATE]
    logp = head[:, STATE:]
    places = position * block_len + jnp.arange(block_len, dtype=jnp.int32)
    first = (places == 0)[None, None, :]
    elems = elements(
        obs,
        logp,
        channel_params,
        present.astype(jnp.float32)[:, None, :],
        frame_keep[:, None, :],
        first,
    )
    grad_local = jnp.einsum(
        "tfw,tfs->ws", hidden, head_cotangent, preferred_element_type=jnp.float32
    )
    local = doubling_prefix(elems, 2)
    totals = tuple(item[:, :, -1].reshape(-1, grad_local.shape[1]) for item in local)
    prefix, head_grad = scan_and_sum(totals, grad_local, ROUNDS)
    prefix = tuple(item.reshape(local[0].shape[:2])[:, :, None] for item in prefix)
    final = combine(prefix, local)
    return (final[1], head_grad)


def solution(mesh):
    devices = mesh.devices.reshape((2,) * (len(TAKE) + len(TIME)))
    fine = jax.sharding.Mesh(devices, TAKE + TIME)
    return jax.shard_map(
        per_device,
        mesh=fine,
        in_specs=(
            P(TAKE, TIME, None),
            P(),
            P(),
            P(),
            P(),
            P(TAKE, TIME),
            P(TAKE, TIME),
            P(),
            P(TAKE, TIME, None),
        ),
        out_specs=(P(TAKE, None, TIME), P()),
        check_vma=False,
    )
```

```python
import jax
import jax.numpy as jnp
from jax import lax
from jax.sharding import PartitionSpec as P

STATE = 64
LAYERS = 3
DMAX = 64
HALO = 136
TIME = ("z3", "z2", "z1", "z0", "xh", "xl", "core")
TAKE = ("th", "tl")


def extended_2(block, sides, width):
    for axis, dim in sides:
        count = lax.axis_size(axis)
        forward = [(i, i + 1) for i in range(count - 1)]
        backward = [(target, source) for source, target in forward]
        low = lax.ppermute(
            lax.slice_in_dim(block, block.shape[dim] - width, None, axis=dim), axis, forward
        )
        high = lax.ppermute(lax.slice_in_dim(block, 0, width, axis=dim), axis, backward)
        block = jnp.concatenate([low, block, high], axis=dim)
    return block


def prefix_2(part, axis, combine, identity):
    place = lax.axis_index(axis)
    gathered = jax.tree.map(lambda a: lax.all_gather(a, axis), part)
    state = jax.tree.map(lambda a, e: jnp.zeros_like(a) + jnp.asarray(e, a.dtype), part, identity)

    def one(turn, state):
        return combine(
            state, jax.tree.map(lambda a: lax.dynamic_index_in_dim(a, turn, 0, False), gathered)
        )

    return lax.fori_loop(0, place, one, state)


def combine(early, late):
    a_one, b_one, c_one, e_one, j_one = early
    a_two, b_two, c_two, e_two, j_two = late
    denom = 1.0 + c_one * j_two
    new_a = a_two * a_one / denom
    new_b = a_two * (b_one + c_one * e_two) / denom + b_two
    new_c = a_two * a_two * c_one / denom + c_two
    new_e = a_one * (e_two - j_two * b_one) / denom + e_one
    new_j = a_one * a_one * j_two / denom + j_one
    return (new_a, new_b, new_c, new_e, new_j)


def doubling_prefix(elems, axis):
    length = elems[0].shape[axis]
    result = elems
    offset = 1
    while offset < length:
        moved = []
        for index, item in enumerate(result):
            fill_value = 1.0 if index == 0 else 0.0
            pad_shape = list(item.shape)
            pad_shape[axis] = offset
            fill = jnp.full(pad_shape, fill_value, item.dtype)
            kept = lax.slice_in_dim(item, 0, length - offset, axis=axis)
            moved.append(jnp.concatenate([fill, kept], axis=axis))
        result = combine(tuple(moved), result)
        offset = offset * 2
    return result


def pair_sum(value, axis):
    return value + lax.ppermute(value, axis, [(0, 1), (1, 0)])


def gather_sum(value, axis):
    slots = lax.all_gather(value, axis)
    total = slots[0]
    for j in range(1, slots.shape[0]):
        total = total + slots[j]
    return total


def scan_and_sum(totals, grad, axes):
    identity = (jnp.ones_like(totals[0]),) + tuple(jnp.zeros_like(item) for item in totals[1:])
    prefix = identity
    rows = grad.shape[0]
    width = totals[0].shape[0]
    for axis in axes:
        digit = lax.axis_index(axis)
        slots = lax.all_gather(jnp.concatenate((grad,) + tuple(totals)), axis)
        radix = slots.shape[0]
        grad = slots[0, :rows]
        for j in range(1, radix):
            grad = grad + slots[j, :rows]
        parts = [
            tuple(slots[j, rows + k * width : rows + (k + 1) * width] for k in range(len(totals)))
            for j in range(radix)
        ]
        earlier = [identity]
        running = parts[0]
        for item in parts[1:]:
            earlier.append(running)
            running = combine(running, item)
        totals = running
        chosen = earlier[0]
        for j in range(1, radix):
            chosen = tuple(jnp.where(digit == j, e, c) for e, c in zip(earlier[j], chosen))
        prefix = combine(chosen, prefix)
    return prefix, grad

def elements(obs, logp, params, present, keep, first):
    rate = params[0][:, None]
    noise = params[1][:, None]
    scale = params[2][:, None]
    trans = jnp.exp(-rate) * keep
    prec = present * scale * jax.nn.softplus(logp)
    denom = 1.0 + noise * prec
    zeros = jnp.zeros_like(obs)
    elem_a = jnp.where(first, zeros, trans / denom)
    elem_b = jnp.where(first, prec * obs / (1.0 + prec), noise * prec * obs / denom)
    elem_c = jnp.where(first, 1.0 / (1.0 + prec), noise / denom)
    elem_e = jnp.where(first, zeros, trans * prec * obs / denom)
    elem_j = jnp.where(first, zeros, trans * trans * prec / denom)
    return (elem_a, elem_b, elem_c, elem_e, elem_j)


def conv_layer(extended, weights, bias, dilation):
    out_len = extended.shape[1] - 2 * DMAX
    acc = jnp.zeros((extended.shape[0], out_len, extended.shape[2]), jnp.float32)
    for tap in range(3):
        piece = lax.dynamic_slice_in_dim(extended, DMAX + (tap - 1) * dilation, out_len, 1)
        acc = acc + jnp.einsum(
            "tfw,wv->tfv", piece, weights[tap], preferred_element_type=jnp.float32
        )
    center = extended[:, DMAX : DMAX + out_len]
    return (center.astype(jnp.float32) + jax.nn.silu(acc + bias[None, None, :])).astype(
        jnp.bfloat16
    )


def per_device(
    frames,
    conv_weight,
    conv_bias,
    dilations,
    head_weight,
    present,
    frame_keep,
    channel_params,
    head_cotangent,
):
    block_len = frames.shape[1]
    position = lax.axis_index(TIME)
    hidden = frames
    halo = HALO
    hidden = extended_2(hidden, ((TIME, 1),), halo)
    count = lax.axis_size(TIME)
    spots = position * block_len - halo + jnp.arange(block_len + 2 * halo, dtype=jnp.int32)
    inside = ((spots >= 0) & (spots < count * block_len))[None, :, None]
    pad = ((0, 0), (DMAX, DMAX), (0, 0))
    for layer in range(LAYERS):
        extended = jnp.pad(hidden, pad)
        hidden = conv_layer(extended, conv_weight[layer], conv_bias[layer], dilations[layer])
        hidden = jnp.where(inside, hidden, jnp.zeros_like(hidden))
    hidden = hidden[:, halo : halo + block_len]
    head = jnp.einsum("tfw,ws->tsf", hidden, head_weight, preferred_element_type=jnp.float32)
    obs = head[:, :STATE]
    logp = head[:, STATE:]
    places = position * block_len + jnp.arange(block_len, dtype=jnp.int32)
    first = (places == 0)[None, None, :]
    elems = elements(
        obs,
        logp,
        channel_params,
        present.astype(jnp.float32)[:, None, :],
        frame_keep[:, None, :],
        first,
    )
    grad_local = jnp.einsum(
        "tfw,tfs->ws", hidden, head_cotangent, preferred_element_type=jnp.float32
    )
    grad_local = pair_sum(pair_sum(grad_local, "tl"), "th")
    local = doubling_prefix(elems, 2)
    totals = tuple(item[:, :, -1].reshape(-1, grad_local.shape[1]) for item in local)
    prefix, head_grad = scan_and_sum(totals, grad_local, TIME[::-1])
    prefix = tuple(item.reshape(local[0].shape[:2])[:, :, None] for item in prefix)
    final = combine(prefix, local)
    return (final[1], head_grad)


def solution(mesh):
    devices = mesh.devices.reshape((2,) * (len(TAKE) + len(TIME)))
    fine = jax.sharding.Mesh(devices, TAKE + TIME)
    return jax.shard_map(
        per_device,
        mesh=fine,
        in_specs=(
            P(TAKE, TIME, None),
            P(),
            P(),
            P(),
            P(),
            P(TAKE, TIME),
            P(TAKE, TIME),
            P(),
            P(TAKE, TIME, None),
        ),
        out_specs=(P(TAKE, None, TIME), P()),
        check_vma=False,
    )
```

```python
import jax
import jax.numpy as jnp
from jax import lax
from jax.sharding import PartitionSpec as P

STATE = 64
LAYERS = 3
DMAX = 64
HALO = 136
TIME = ("z3", "z2", "z1", "z0", "xh", "xl", "core")
TAKE = ("th", "tl")


def extended_2(block, sides, width):
    for axis, dim in sides:
        count = lax.axis_size(axis)
        forward = [(i, i + 1) for i in range(count - 1)]
        backward = [(target, source) for source, target in forward]
        low = lax.ppermute(
            lax.slice_in_dim(block, block.shape[dim] - width, None, axis=dim), axis, forward
        )
        high = lax.ppermute(lax.slice_in_dim(block, 0, width, axis=dim), axis, backward)
        block = jnp.concatenate([low, block, high], axis=dim)
    return block


def prefix_2(part, axis, combine, identity):
    place = lax.axis_index(axis)
    gathered = jax.tree.map(lambda a: lax.all_gather(a, axis), part)
    state = jax.tree.map(lambda a, e: jnp.zeros_like(a) + jnp.asarray(e, a.dtype), part, identity)

    def one(turn, state):
        return combine(
            state, jax.tree.map(lambda a: lax.dynamic_index_in_dim(a, turn, 0, False), gathered)
        )

    return lax.fori_loop(0, place, one, state)


def combine(early, late):
    a_one, b_one, c_one, e_one, j_one = early
    a_two, b_two, c_two, e_two, j_two = late
    denom = 1.0 + c_one * j_two
    new_a = a_two * a_one / denom
    new_b = a_two * (b_one + c_one * e_two) / denom + b_two
    new_c = a_two * a_two * c_one / denom + c_two
    new_e = a_one * (e_two - j_two * b_one) / denom + e_one
    new_j = a_one * a_one * j_two / denom + j_one
    return (new_a, new_b, new_c, new_e, new_j)


def doubling_prefix(elems, axis):
    length = elems[0].shape[axis]
    result = elems
    offset = 1
    while offset < length:
        moved = []
        for index, item in enumerate(result):
            fill_value = 1.0 if index == 0 else 0.0
            pad_shape = list(item.shape)
            pad_shape[axis] = offset
            fill = jnp.full(pad_shape, fill_value, item.dtype)
            kept = lax.slice_in_dim(item, 0, length - offset, axis=axis)
            moved.append(jnp.concatenate([fill, kept], axis=axis))
        result = combine(tuple(moved), result)
        offset = offset * 2
    return result


def pair_sum(value, axis):
    return value + lax.ppermute(value, axis, [(0, 1), (1, 0)])


def gather_sum(value, axis):
    slots = lax.all_gather(value, axis)
    total = slots[0]
    for j in range(1, slots.shape[0]):
        total = total + slots[j]
    return total


def scan_and_sum(totals, grad, axes):
    identity = (jnp.ones_like(totals[0]),) + tuple(jnp.zeros_like(item) for item in totals[1:])
    prefix = identity
    rows = grad.shape[0]
    width = totals[0].shape[0]
    for axis in axes:
        digit = lax.axis_index(axis)
        packed = jnp.concatenate((grad,) + tuple(totals))
        if axis in ("z2", "z3"):
            other = lax.ppermute(packed, axis, [(0, 1), (1, 0)])
            low = jnp.where(digit == 0, packed, other)
            high = jnp.where(digit == 0, other, packed)
            slots = jnp.stack([low, high])
        else:
            slots = lax.all_gather(packed, axis)
        radix = slots.shape[0]
        grad = slots[0, :rows]
        for j in range(1, radix):
            grad = grad + slots[j, :rows]
        parts = [
            tuple(slots[j, rows + k * width : rows + (k + 1) * width] for k in range(len(totals)))
            for j in range(radix)
        ]
        earlier = [identity]
        running = parts[0]
        for item in parts[1:]:
            earlier.append(running)
            running = combine(running, item)
        totals = running
        chosen = earlier[0]
        for j in range(1, radix):
            chosen = tuple(jnp.where(digit == j, e, c) for e, c in zip(earlier[j], chosen))
        prefix = combine(chosen, prefix)
    return prefix, grad

def elements(obs, logp, params, present, keep, first):
    rate = params[0][:, None]
    noise = params[1][:, None]
    scale = params[2][:, None]
    trans = jnp.exp(-rate) * keep
    prec = present * scale * jax.nn.softplus(logp)
    denom = 1.0 + noise * prec
    zeros = jnp.zeros_like(obs)
    elem_a = jnp.where(first, zeros, trans / denom)
    elem_b = jnp.where(first, prec * obs / (1.0 + prec), noise * prec * obs / denom)
    elem_c = jnp.where(first, 1.0 / (1.0 + prec), noise / denom)
    elem_e = jnp.where(first, zeros, trans * prec * obs / denom)
    elem_j = jnp.where(first, zeros, trans * trans * prec / denom)
    return (elem_a, elem_b, elem_c, elem_e, elem_j)


def conv_layer(extended, weights, bias, dilation):
    out_len = extended.shape[1] - 2 * DMAX
    acc = jnp.zeros((extended.shape[0], out_len, extended.shape[2]), jnp.float32)
    for tap in range(3):
        piece = lax.dynamic_slice_in_dim(extended, DMAX + (tap - 1) * dilation, out_len, 1)
        acc = acc + jnp.einsum(
            "tfw,wv->tfv", piece, weights[tap], preferred_element_type=jnp.float32
        )
    center = extended[:, DMAX : DMAX + out_len]
    return (center.astype(jnp.float32) + jax.nn.silu(acc + bias[None, None, :])).astype(
        jnp.bfloat16
    )


def per_device(
    frames,
    conv_weight,
    conv_bias,
    dilations,
    head_weight,
    present,
    frame_keep,
    channel_params,
    head_cotangent,
):
    block_len = frames.shape[1]
    position = lax.axis_index(TIME)
    hidden = frames
    halo = HALO
    hidden = extended_2(hidden, ((TIME, 1),), halo)
    count = lax.axis_size(TIME)
    spots = position * block_len - halo + jnp.arange(block_len + 2 * halo, dtype=jnp.int32)
    inside = ((spots >= 0) & (spots < count * block_len))[None, :, None]
    pad = ((0, 0), (DMAX, DMAX), (0, 0))
    for layer in range(LAYERS):
        extended = jnp.pad(hidden, pad)
        hidden = conv_layer(extended, conv_weight[layer], conv_bias[layer], dilations[layer])
        hidden = jnp.where(inside, hidden, jnp.zeros_like(hidden))
    hidden = hidden[:, halo : halo + block_len]
    head = jnp.einsum("tfw,ws->tsf", hidden, head_weight, preferred_element_type=jnp.float32)
    obs = head[:, :STATE]
    logp = head[:, STATE:]
    places = position * block_len + jnp.arange(block_len, dtype=jnp.int32)
    first = (places == 0)[None, None, :]
    elems = elements(
        obs,
        logp,
        channel_params,
        present.astype(jnp.float32)[:, None, :],
        frame_keep[:, None, :],
        first,
    )
    grad_local = jnp.einsum(
        "tfw,tfs->ws", hidden, head_cotangent, preferred_element_type=jnp.float32
    )
    grad_local = pair_sum(pair_sum(grad_local, "tl"), "th")
    local = doubling_prefix(elems, 2)
    totals = tuple(item[:, :, -1].reshape(-1, grad_local.shape[1]) for item in local)
    prefix, head_grad = scan_and_sum(totals, grad_local, TIME[::-1])
    prefix = tuple(item.reshape(local[0].shape[:2])[:, :, None] for item in prefix)
    final = combine(prefix, local)
    return (final[1], head_grad)


def solution(mesh):
    devices = mesh.devices.reshape((2,) * (len(TAKE) + len(TIME)))
    fine = jax.sharding.Mesh(devices, TAKE + TIME)
    return jax.shard_map(
        per_device,
        mesh=fine,
        in_specs=(
            P(TAKE, TIME, None),
            P(),
            P(),
            P(),
            P(),
            P(TAKE, TIME),
            P(TAKE, TIME),
            P(),
            P(TAKE, TIME, None),
        ),
        out_specs=(P(TAKE, None, TIME), P()),
        check_vma=False,
    )
```

```python
import jax
import jax.numpy as jnp
from jax import lax
from jax.sharding import PartitionSpec as P

STATE = 64
LAYERS = 3
DMAX = 64
HALO = LAYERS * DMAX
TIME = ("z3", "z2", "z1", "z0", "xh", "xl", "core")
TAKE = ("th", "tl")


def extended_2(block, sides, width):
    for axis, dim in sides:
        count = lax.axis_size(axis)
        forward = [(i, i + 1) for i in range(count - 1)]
        backward = [(target, source) for source, target in forward]
        low = lax.ppermute(
            lax.slice_in_dim(block, block.shape[dim] - width, None, axis=dim), axis, forward
        )
        high = lax.ppermute(lax.slice_in_dim(block, 0, width, axis=dim), axis, backward)
        block = jnp.concatenate([low, block, high], axis=dim)
    return block


def prefix_2(part, axis, combine, identity):
    place = lax.axis_index(axis)
    gathered = jax.tree.map(lambda a: lax.all_gather(a, axis), part)
    state = jax.tree.map(lambda a, e: jnp.zeros_like(a) + jnp.asarray(e, a.dtype), part, identity)

    def one(turn, state):
        return combine(
            state, jax.tree.map(lambda a: lax.dynamic_index_in_dim(a, turn, 0, False), gathered)
        )

    return lax.fori_loop(0, place, one, state)


def combine(early, late):
    a_one, b_one, c_one, e_one, j_one = early
    a_two, b_two, c_two, e_two, j_two = late
    denom = 1.0 + c_one * j_two
    new_a = a_two * a_one / denom
    new_b = a_two * (b_one + c_one * e_two) / denom + b_two
    new_c = a_two * a_two * c_one / denom + c_two
    new_e = a_one * (e_two - j_two * b_one) / denom + e_one
    new_j = a_one * a_one * j_two / denom + j_one
    return (new_a, new_b, new_c, new_e, new_j)


def doubling_prefix(elems, axis):
    length = elems[0].shape[axis]
    result = elems
    offset = 1
    while offset < length:
        moved = []
        for index, item in enumerate(result):
            fill_value = 1.0 if index == 0 else 0.0
            pad_shape = list(item.shape)
            pad_shape[axis] = offset
            fill = jnp.full(pad_shape, fill_value, item.dtype)
            kept = lax.slice_in_dim(item, 0, length - offset, axis=axis)
            moved.append(jnp.concatenate([fill, kept], axis=axis))
        result = combine(tuple(moved), result)
        offset = offset * 2
    return result


def pair_sum(value, axis):
    return value + lax.ppermute(value, axis, [(0, 1), (1, 0)])


def gather_sum(value, axis):
    slots = lax.all_gather(value, axis)
    total = slots[0]
    for j in range(1, slots.shape[0]):
        total = total + slots[j]
    return total


def scan_and_sum(totals, grad, axes):
    identity = (jnp.ones_like(totals[0]),) + tuple(jnp.zeros_like(item) for item in totals[1:])
    prefix = identity
    rows = grad.shape[0]
    width = totals[0].shape[0]
    for axis in axes:
        digit = lax.axis_index(axis)
        slots = lax.all_gather(jnp.concatenate((grad,) + tuple(totals)), axis)
        radix = slots.shape[0]
        grad = slots[0, :rows]
        for j in range(1, radix):
            grad = grad + slots[j, :rows]
        parts = [
            tuple(slots[j, rows + k * width : rows + (k + 1) * width] for k in range(len(totals)))
            for j in range(radix)
        ]
        earlier = [identity]
        running = parts[0]
        for item in parts[1:]:
            earlier.append(running)
            running = combine(running, item)
        totals = running
        chosen = earlier[0]
        for j in range(1, radix):
            chosen = tuple(jnp.where(digit == j, e, c) for e, c in zip(earlier[j], chosen))
        prefix = combine(chosen, prefix)
    return prefix, grad

def elements(obs, logp, params, present, keep, first):
    rate = params[0][:, None]
    noise = params[1][:, None]
    scale = params[2][:, None]
    trans = jnp.exp(-rate) * keep
    prec = present * scale * jax.nn.softplus(logp)
    denom = 1.0 + noise * prec
    zeros = jnp.zeros_like(obs)
    elem_a = jnp.where(first, zeros, trans / denom)
    elem_b = jnp.where(first, prec * obs / (1.0 + prec), noise * prec * obs / denom)
    elem_c = jnp.where(first, 1.0 / (1.0 + prec), noise / denom)
    elem_e = jnp.where(first, zeros, trans * prec * obs / denom)
    elem_j = jnp.where(first, zeros, trans * trans * prec / denom)
    return (elem_a, elem_b, elem_c, elem_e, elem_j)


def conv_layer(extended, weights, bias, dilation):
    out_len = extended.shape[1] - 2 * DMAX
    acc = jnp.zeros((extended.shape[0], out_len, extended.shape[2]), jnp.float32)
    for tap in range(3):
        piece = lax.dynamic_slice_in_dim(extended, DMAX + (tap - 1) * dilation, out_len, 1)
        acc = acc + jnp.einsum(
            "tfw,wv->tfv", piece, weights[tap], preferred_element_type=jnp.float32
        )
    center = extended[:, DMAX : DMAX + out_len]
    return (center.astype(jnp.float32) + jax.nn.silu(acc + bias[None, None, :])).astype(
        jnp.bfloat16
    )


def per_device(
    frames,
    conv_weight,
    conv_bias,
    dilations,
    head_weight,
    present,
    frame_keep,
    channel_params,
    head_cotangent,
):
    block_len = frames.shape[1]
    position = lax.axis_index(TIME)
    hidden = frames
    halo = HALO
    hidden = extended_2(hidden, ((TIME, 1),), halo)
    count = lax.axis_size(TIME)
    for layer in range(LAYERS):
        hidden = conv_layer(hidden, conv_weight[layer], conv_bias[layer], dilations[layer])
        start = position * block_len - halo + (layer + 1) * DMAX
        spots = start + jnp.arange(hidden.shape[1], dtype=jnp.int32)
        inside = ((spots >= 0) & (spots < count * block_len))[None, :, None]
        hidden = jnp.where(inside, hidden, jnp.zeros_like(hidden))
    head = jnp.einsum("tfw,ws->tsf", hidden, head_weight, preferred_element_type=jnp.float32)
    obs = head[:, :STATE]
    logp = head[:, STATE:]
    places = position * block_len + jnp.arange(block_len, dtype=jnp.int32)
    first = (places == 0)[None, None, :]
    elems = elements(
        obs,
        logp,
        channel_params,
        present.astype(jnp.float32)[:, None, :],
        frame_keep[:, None, :],
        first,
    )
    grad_local = jnp.einsum(
        "tfw,tfs->ws", hidden, head_cotangent, preferred_element_type=jnp.float32
    )
    grad_local = pair_sum(pair_sum(grad_local, "tl"), "th")
    local = doubling_prefix(elems, 2)
    totals = tuple(item[:, :, -1].reshape(-1, grad_local.shape[1]) for item in local)
    prefix, head_grad = scan_and_sum(totals, grad_local, TIME[::-1])
    prefix = tuple(item.reshape(local[0].shape[:2])[:, :, None] for item in prefix)
    final = combine(prefix, local)
    return (final[1], head_grad)


def solution(mesh):
    devices = mesh.devices.reshape((2,) * (len(TAKE) + len(TIME)))
    fine = jax.sharding.Mesh(devices, TAKE + TIME)
    return jax.shard_map(
        per_device,
        mesh=fine,
        in_specs=(
            P(TAKE, TIME, None),
            P(),
            P(),
            P(),
            P(),
            P(TAKE, TIME),
            P(TAKE, TIME),
            P(),
            P(TAKE, TIME, None),
        ),
        out_specs=(P(TAKE, None, TIME), P()),
        check_vma=False,
    )
```

```python
import jax
import jax.numpy as jnp
from jax import lax
from jax.sharding import PartitionSpec as P

STATE = 64
LAYERS = 3
DMAX = 64
HALO = 130
TIME = ("z3", "z2", "z1", "z0", "xh", "xl", "core")
TAKE = ("th", "tl")


def extended_2(block, sides, width):
    for axis, dim in sides:
        count = lax.axis_size(axis)
        forward = [(i, i + 1) for i in range(count - 1)]
        backward = [(target, source) for source, target in forward]
        low = lax.ppermute(
            lax.slice_in_dim(block, block.shape[dim] - width, None, axis=dim), axis, forward
        )
        high = lax.ppermute(lax.slice_in_dim(block, 0, width, axis=dim), axis, backward)
        block = jnp.concatenate([low, block, high], axis=dim)
    return block


def prefix_2(part, axis, combine, identity):
    place = lax.axis_index(axis)
    gathered = jax.tree.map(lambda a: lax.all_gather(a, axis), part)
    state = jax.tree.map(lambda a, e: jnp.zeros_like(a) + jnp.asarray(e, a.dtype), part, identity)

    def one(turn, state):
        return combine(
            state, jax.tree.map(lambda a: lax.dynamic_index_in_dim(a, turn, 0, False), gathered)
        )

    return lax.fori_loop(0, place, one, state)


def combine(early, late):
    a_one, b_one, c_one, e_one, j_one = early
    a_two, b_two, c_two, e_two, j_two = late
    denom = 1.0 + c_one * j_two
    new_a = a_two * a_one / denom
    new_b = a_two * (b_one + c_one * e_two) / denom + b_two
    new_c = a_two * a_two * c_one / denom + c_two
    new_e = a_one * (e_two - j_two * b_one) / denom + e_one
    new_j = a_one * a_one * j_two / denom + j_one
    return (new_a, new_b, new_c, new_e, new_j)


def doubling_prefix(elems, axis):
    length = elems[0].shape[axis]
    result = elems
    offset = 1
    while offset < length:
        moved = []
        for index, item in enumerate(result):
            fill_value = 1.0 if index == 0 else 0.0
            pad_shape = list(item.shape)
            pad_shape[axis] = offset
            fill = jnp.full(pad_shape, fill_value, item.dtype)
            kept = lax.slice_in_dim(item, 0, length - offset, axis=axis)
            moved.append(jnp.concatenate([fill, kept], axis=axis))
        result = combine(tuple(moved), result)
        offset = offset * 2
    return result


def pair_sum(value, axis):
    return value + lax.ppermute(value, axis, [(0, 1), (1, 0)])


def gather_sum(value, axis):
    slots = lax.all_gather(value, axis)
    total = slots[0]
    for j in range(1, slots.shape[0]):
        total = total + slots[j]
    return total


def scan_and_sum(totals, grad, axes):
    identity = (jnp.ones_like(totals[0]),) + tuple(jnp.zeros_like(item) for item in totals[1:])
    prefix = identity
    rows = grad.shape[0]
    width = totals[0].shape[0]
    for axis in axes:
        digit = lax.axis_index(axis)
        slots = lax.all_gather(jnp.concatenate((grad,) + tuple(totals)), axis)
        radix = slots.shape[0]
        grad = slots[0, :rows]
        for j in range(1, radix):
            grad = grad + slots[j, :rows]
        parts = [
            tuple(slots[j, rows + k * width : rows + (k + 1) * width] for k in range(len(totals)))
            for j in range(radix)
        ]
        earlier = [identity]
        running = parts[0]
        for item in parts[1:]:
            earlier.append(running)
            running = combine(running, item)
        totals = running
        chosen = earlier[0]
        for j in range(1, radix):
            chosen = tuple(jnp.where(digit == j, e, c) for e, c in zip(earlier[j], chosen))
        prefix = combine(chosen, prefix)
    return prefix, grad

def elements(obs, logp, params, present, keep, first):
    rate = params[0][:, None]
    noise = params[1][:, None]
    scale = params[2][:, None]
    trans = jnp.exp(-rate) * keep
    prec = present * scale * jax.nn.softplus(logp)
    denom = 1.0 + noise * prec
    zeros = jnp.zeros_like(obs)
    elem_a = jnp.where(first, zeros, trans / denom)
    elem_b = jnp.where(first, prec * obs / (1.0 + prec), noise * prec * obs / denom)
    elem_c = jnp.where(first, 1.0 / (1.0 + prec), noise / denom)
    elem_e = jnp.where(first, zeros, trans * prec * obs / denom)
    elem_j = jnp.where(first, zeros, trans * trans * prec / denom)
    return (elem_a, elem_b, elem_c, elem_e, elem_j)


def conv_layer(extended, weights, bias, dilation):
    out_len = extended.shape[1] - 2 * DMAX
    acc = jnp.zeros((extended.shape[0], out_len, extended.shape[2]), jnp.float32)
    for tap in range(3):
        piece = lax.dynamic_slice_in_dim(extended, DMAX + (tap - 1) * dilation, out_len, 1)
        acc = acc + jnp.einsum(
            "tfw,wv->tfv", piece, weights[tap], preferred_element_type=jnp.float32
        )
    center = extended[:, DMAX : DMAX + out_len]
    return (center.astype(jnp.float32) + jax.nn.silu(acc + bias[None, None, :])).astype(
        jnp.bfloat16
    )


def per_device(
    frames,
    conv_weight,
    conv_bias,
    dilations,
    head_weight,
    present,
    frame_keep,
    channel_params,
    head_cotangent,
):
    block_len = frames.shape[1]
    position = lax.axis_index(TIME)
    hidden = frames
    halo = HALO
    hidden = extended_2(hidden, ((TIME, 1),), halo)
    count = lax.axis_size(TIME)
    spots = position * block_len - halo + jnp.arange(block_len + 2 * halo, dtype=jnp.int32)
    inside = ((spots >= 0) & (spots < count * block_len))[None, :, None]
    pad = ((0, 0), (DMAX, DMAX), (0, 0))
    for layer in range(LAYERS):
        extended = jnp.pad(hidden, pad)
        hidden = conv_layer(extended, conv_weight[layer], conv_bias[layer], dilations[layer])
        hidden = jnp.where(inside, hidden, jnp.zeros_like(hidden))
    hidden = hidden[:, halo : halo + block_len]
    head = jnp.einsum("tfw,ws->tsf", hidden, head_weight, preferred_element_type=jnp.float32)
    obs = head[:, :STATE]
    logp = head[:, STATE:]
    places = position * block_len + jnp.arange(block_len, dtype=jnp.int32)
    first = (places == 0)[None, None, :]
    elems = elements(
        obs,
        logp,
        channel_params,
        present.astype(jnp.float32)[:, None, :],
        frame_keep[:, None, :],
        first,
    )
    grad_local = jnp.einsum(
        "tfw,tfs->ws", hidden, head_cotangent, preferred_element_type=jnp.float32
    )
    grad_local = pair_sum(pair_sum(grad_local, "tl"), "th")
    local = doubling_prefix(elems, 2)
    totals = tuple(item[:, :, -1].reshape(-1, grad_local.shape[1]) for item in local)
    prefix, head_grad = scan_and_sum(totals, grad_local, TIME[::-1])
    prefix = tuple(item.reshape(local[0].shape[:2])[:, :, None] for item in prefix)
    final = combine(prefix, local)
    return (final[1], head_grad)


def solution(mesh):
    devices = mesh.devices.reshape((2,) * (len(TAKE) + len(TIME)))
    fine = jax.sharding.Mesh(devices, TAKE + TIME)
    return jax.shard_map(
        per_device,
        mesh=fine,
        in_specs=(
            P(TAKE, TIME, None),
            P(),
            P(),
            P(),
            P(),
            P(TAKE, TIME),
            P(TAKE, TIME),
            P(),
            P(TAKE, TIME, None),
        ),
        out_specs=(P(TAKE, None, TIME), P()),
        check_vma=False,
    )
```

```python
import jax
import jax.numpy as jnp
from jax import lax
from jax.sharding import PartitionSpec as P

STATE = 64
LAYERS = 3
DMAX = 64
HALO = 144
TIME = ("z3", "z2", "z1", "z0", "xh", "xl", "core")
TAKE = ("th", "tl")


def extended_2(block, sides, width):
    for axis, dim in sides:
        count = lax.axis_size(axis)
        forward = [(i, i + 1) for i in range(count - 1)]
        backward = [(target, source) for source, target in forward]
        low = lax.ppermute(
            lax.slice_in_dim(block, block.shape[dim] - width, None, axis=dim), axis, forward
        )
        high = lax.ppermute(lax.slice_in_dim(block, 0, width, axis=dim), axis, backward)
        block = jnp.concatenate([low, block, high], axis=dim)
    return block


def prefix_2(part, axis, combine, identity):
    place = lax.axis_index(axis)
    gathered = jax.tree.map(lambda a: lax.all_gather(a, axis), part)
    state = jax.tree.map(lambda a, e: jnp.zeros_like(a) + jnp.asarray(e, a.dtype), part, identity)

    def one(turn, state):
        return combine(
            state, jax.tree.map(lambda a: lax.dynamic_index_in_dim(a, turn, 0, False), gathered)
        )

    return lax.fori_loop(0, place, one, state)


def combine(early, late):
    a_one, b_one, c_one, e_one, j_one = early
    a_two, b_two, c_two, e_two, j_two = late
    denom = 1.0 + c_one * j_two
    new_a = a_two * a_one / denom
    new_b = a_two * (b_one + c_one * e_two) / denom + b_two
    new_c = a_two * a_two * c_one / denom + c_two
    new_e = a_one * (e_two - j_two * b_one) / denom + e_one
    new_j = a_one * a_one * j_two / denom + j_one
    return (new_a, new_b, new_c, new_e, new_j)


def doubling_prefix(elems, axis):
    length = elems[0].shape[axis]
    result = elems
    offset = 1
    while offset < length:
        moved = []
        for index, item in enumerate(result):
            fill_value = 1.0 if index == 0 else 0.0
            pad_shape = list(item.shape)
            pad_shape[axis] = offset
            fill = jnp.full(pad_shape, fill_value, item.dtype)
            kept = lax.slice_in_dim(item, 0, length - offset, axis=axis)
            moved.append(jnp.concatenate([fill, kept], axis=axis))
        result = combine(tuple(moved), result)
        offset = offset * 2
    return result


def pair_sum(value, axis):
    return value + lax.ppermute(value, axis, [(0, 1), (1, 0)])


def gather_sum(value, axis):
    slots = lax.all_gather(value, axis)
    total = slots[0]
    for j in range(1, slots.shape[0]):
        total = total + slots[j]
    return total


def scan_and_sum(totals, grad, axes):
    identity = (jnp.ones_like(totals[0]),) + tuple(jnp.zeros_like(item) for item in totals[1:])
    prefix = identity
    rows = grad.shape[0]
    width = totals[0].shape[0]
    for axis in axes:
        digit = lax.axis_index(axis)
        slots = lax.all_gather(jnp.concatenate((grad,) + tuple(totals)), axis)
        radix = slots.shape[0]
        grad = slots[0, :rows]
        for j in range(1, radix):
            grad = grad + slots[j, :rows]
        parts = [
            tuple(slots[j, rows + k * width : rows + (k + 1) * width] for k in range(len(totals)))
            for j in range(radix)
        ]
        earlier = [identity]
        running = parts[0]
        for item in parts[1:]:
            earlier.append(running)
            running = combine(running, item)
        totals = running
        chosen = earlier[0]
        for j in range(1, radix):
            chosen = tuple(jnp.where(digit == j, e, c) for e, c in zip(earlier[j], chosen))
        prefix = combine(chosen, prefix)
    return prefix, grad

def elements(obs, logp, params, present, keep, first):
    rate = params[0][:, None]
    noise = params[1][:, None]
    scale = params[2][:, None]
    trans = jnp.exp(-rate) * keep
    prec = present * scale * jax.nn.softplus(logp)
    denom = 1.0 + noise * prec
    zeros = jnp.zeros_like(obs)
    elem_a = jnp.where(first, zeros, trans / denom)
    elem_b = jnp.where(first, prec * obs / (1.0 + prec), noise * prec * obs / denom)
    elem_c = jnp.where(first, 1.0 / (1.0 + prec), noise / denom)
    elem_e = jnp.where(first, zeros, trans * prec * obs / denom)
    elem_j = jnp.where(first, zeros, trans * trans * prec / denom)
    return (elem_a, elem_b, elem_c, elem_e, elem_j)


def conv_layer(extended, weights, bias, dilation):
    out_len = extended.shape[1] - 2 * DMAX
    acc = jnp.zeros((extended.shape[0], out_len, extended.shape[2]), jnp.float32)
    for tap in range(3):
        piece = lax.dynamic_slice_in_dim(extended, DMAX + (tap - 1) * dilation, out_len, 1)
        acc = acc + jnp.einsum(
            "tfw,wv->tfv", piece, weights[tap], preferred_element_type=jnp.float32
        )
    center = extended[:, DMAX : DMAX + out_len]
    return (center.astype(jnp.float32) + jax.nn.silu(acc + bias[None, None, :])).astype(
        jnp.bfloat16
    )


def per_device(
    frames,
    conv_weight,
    conv_bias,
    dilations,
    head_weight,
    present,
    frame_keep,
    channel_params,
    head_cotangent,
):
    block_len = frames.shape[1]
    position = lax.axis_index(TIME)
    hidden = frames
    halo = HALO
    hidden = extended_2(hidden, ((TIME, 1),), halo)
    count = lax.axis_size(TIME)
    spots = position * block_len - halo + jnp.arange(block_len + 2 * halo, dtype=jnp.int32)
    inside = ((spots >= 0) & (spots < count * block_len))[None, :, None]
    pad = ((0, 0), (DMAX, DMAX), (0, 0))
    for layer in range(LAYERS):
        extended = jnp.pad(hidden, pad)
        hidden = conv_layer(extended, conv_weight[layer], conv_bias[layer], dilations[layer])
        hidden = jnp.where(inside, hidden, jnp.zeros_like(hidden))
    hidden = hidden[:, halo : halo + block_len]
    head = jnp.einsum("tfw,ws->tsf", hidden, head_weight, preferred_element_type=jnp.float32)
    obs = head[:, :STATE]
    logp = head[:, STATE:]
    places = position * block_len + jnp.arange(block_len, dtype=jnp.int32)
    first = (places == 0)[None, None, :]
    elems = elements(
        obs,
        logp,
        channel_params,
        present.astype(jnp.float32)[:, None, :],
        frame_keep[:, None, :],
        first,
    )
    grad_local = jnp.einsum(
        "tfw,tfs->ws", hidden, head_cotangent, preferred_element_type=jnp.float32
    )
    grad_local = pair_sum(pair_sum(grad_local, "tl"), "th")
    local = doubling_prefix(elems, 2)
    totals = tuple(item[:, :, -1].reshape(-1, grad_local.shape[1]) for item in local)
    prefix, head_grad = scan_and_sum(totals, grad_local, TIME[::-1])
    prefix = tuple(item.reshape(local[0].shape[:2])[:, :, None] for item in prefix)
    final = combine(prefix, local)
    return (final[1], head_grad)


def solution(mesh):
    devices = mesh.devices.reshape((2,) * (len(TAKE) + len(TIME)))
    fine = jax.sharding.Mesh(devices, TAKE + TIME)
    return jax.shard_map(
        per_device,
        mesh=fine,
        in_specs=(
            P(TAKE, TIME, None),
            P(),
            P(),
            P(),
            P(),
            P(TAKE, TIME),
            P(TAKE, TIME),
            P(),
            P(TAKE, TIME, None),
        ),
        out_specs=(P(TAKE, None, TIME), P()),
        check_vma=False,
    )
```
